128 devices in a mesh: req: 16 (over z, x), head: 8 (over y, core).
Axes of the slice: x: 4, y: 4, z: 4, core: 2. Of those that a mesh axis runs over, the one named last changes fastest.
Arguments:
- tokens: bfloat16 [256, 1280], P('req'), may hold values from -6 to 6
- w_qkv: bfloat16 [2, 3, 1280, 1280], P(None, None, 'head'), may hold values from -0.15625 to 0.15625
- w_out: bfloat16 [2, 1280, 1280], P(None, 'head'), may hold values from -0.15625 to 0.15625
- w_up: bfloat16 [2, 1280, 1280], P(None, 'head'), may hold values from -0.15625 to 0.15625
- w_down: bfloat16 [2, 1280, 1280], P(None, 'head'), may hold values from -0.15625 to 0.15625
- gain_attn: float32 [2, 1280], replicated, may hold values from 0.1 to 1.9
- gain_mlp: float32 [2, 1280], replicated, may hold values from 0.1 to 1.9
- suffix_cache: bfloat16 [2, 2, 512, 1280, 128], P(None, None, 'req', 'head'), may hold values from -110 to 110
- prompt_cache: bfloat16 [2, 2, 96, 1280, 128], P(None, None, 'req', 'head'), may hold values from -110 to 110
- suffix_table: int32 [16, 32], P('req'), may hold values from 0 to 31, each once within a row
- prompt_owner: int32 [96], replicated, may hold values from 0 to 95, each once
- suffix_len: int32 [256], P('req'), may hold values from 1 to 256, 32768 in all
- group_id: int32 [256], P('req'), may hold values from 0 to 23, never falling along the last dimension, each value on 1 to 16 neighbouring positions
Outputs:
- hidden: bfloat16 [256, 1280], P('req')
- new_cache: bfloat16 [2, 2, 256, 1280], P(None, None, 'req', 'head')
The draws below stay inside these ranges and needn't reach their ends.
Inputs may be any that keep to these rules, and one draw needn't show every extreme that they name: `suffix_table`: each row holds every number once. `prompt_owner`: each number once. `group_id`: never falls from one request to the next; every group has 1 to 16 requests, one group exactly 16.
All inputs are finite; a program needn't handle non-finite values. No bound on the sum of `suffix_len` on one device may be relied on, other than what follows from the above.
Results may differ from the reference program's by a relative error of at most 0.019.
The reference program's roundings to bfloat16 on the way count: a program that leaves them out, or rounds other values in their place, can miss the bound.
Values may be sent and summed in bfloat16 or wider, within the bound.
No kernel may reach another device: no remote copies, remote signals or barrier semaphores. Data moves between devices by JAX's collectives and lax.ppermute only.
A program may use at most 128 MiB of HBM per device.

```python
import math
import jax
import jax.numpy as jnp
import numpy as np
from jax import lax

D = 1280
H = 16
HD = 80
FF = 1280
L = 2
PAGE = 128
PPAGES = 4
SPAGES = 2
REQ_DEV = 16
REQS = 256
NGROUPS = 24
PROMPT_PAGES = 96
POOL_DEV = 32
POOL = 512
HH = 1280
N_REQ = 16


def cache_law(key, pages):
    shape = (L, 2, pages, H * HD, PAGE)
    first = jax.random.fold_in(key, 0)
    entries = jnp.clip(jax.random.normal(first, shape, jnp.float32), -6.0, 6.0)
    return entries.astype(jnp.bfloat16)


def draw_suffix_cache(key, part):
    return cache_law(jax.random.fold_in(key, 11), POOL)


def draw_prompt_cache(key, part):
    return cache_law(jax.random.fold_in(key, 23), PROMPT_PAGES)


def shard_levels(key, shape, shards, smallest, high):
    def one(position, shards_of):
        draws = jax.random.uniform(jax.random.fold_in(jax.random.fold_in(key, 6), position), (shards_of,), jnp.float32, smallest / len(shards), high / len(shards))
        return jnp.repeat(jnp.exp(draws), shape[position] // shards_of).reshape((-1,) + (1,) * (len(shape) - position - 1))

    gain = one(*shards[0])
    for cut in shards[1:]:
        gain = gain * one(*cut)
    return gain


def length_profile(count, total, most, skew):
    weights = [(1 << 20) // math.isqrt(rank ** skew) + 1 for rank in range(2, count + 1)]
    spare, given = total - most - (count - 1), [1] * (count - 1)
    while spare > 0:
        free = [i for i in range(count - 1) if given[i] < most]
        whole, left = sum([weights[i] for i in free]), spare
        for i in free:
            extra = min(most - given[i], max(1, left * weights[i] // whole), spare)
            given[i] = given[i] + extra
            spare = spare - extra
    return np.array([most] + given)


def uneven(stream_key, count, total, reach, skew):
    if count == 2:
        one = jax.random.randint(stream_key, (), max(1, total - reach), min(reach, total - 1) + 1)
        return jnp.stack([one, total - one])
    tallies = jnp.asarray(length_profile(count, total, reach, skew), jnp.int32)
    couples = (count - 1) // 2
    giver, sink = tallies[1:1 + 2 * couples:2], tallies[2:2 + 2 * couples:2]
    slack = jnp.minimum(giver - 1, reach - sink)
    passed = jax.random.randint(jax.random.fold_in(stream_key, 1), (couples,), 0, 1 << 20) % (slack + 1)
    tallies = tallies.at[1:1 + 2 * couples:2].set(giver - passed).at[2:2 + 2 * couples:2].set(sink + passed)
    return tallies[jax.random.permutation(jax.random.fold_in(stream_key, 2), count)]


def gaussian(key, extent, deviation, bound, shards=(), held_as=jnp.bfloat16):
    factor_of = shard_levels(key, extent, shards, -0.22, 0.18) if shards else 1.0
    values = jax.random.normal(key, extent, jnp.float32) * deviation * factor_of
    return jnp.minimum(jnp.maximum(values, -bound), bound).astype(held_as)


def setup_inputs(seed: int = 0) -> dict:
    splits = jax.random.split(jax.random.key(seed), 14)
    return {
        "tokens": gaussian(splits[0], (REQS, D), 1.0, 6.0, ((0, 16),)),
        "w_qkv": gaussian(splits[1], (L, 3, HH, D), D ** -0.5, 0.15625, ((2, 8),)),
        "w_out": gaussian(splits[2], (L, HH, D), HH ** -0.5, 0.15625, ((1, 8),)),
        "w_up": gaussian(splits[3], (L, FF, D), D ** -0.5, 0.15625, ((1, 8),)),
        "w_down": gaussian(splits[4], (L, FF, D), FF ** -0.5, 0.15625, ((1, 8),)),
        "gain_attn": jnp.clip(1.0 + 0.18 * jax.random.normal(splits[5], (L, D), jnp.float32), 0.1, 1.9),
        "gain_mlp": jnp.clip(1.0 + 0.18 * jax.random.normal(splits[6], (L, D), jnp.float32), 0.1, 1.9),
        "suffix_cache": draw_suffix_cache(jax.random.fold_in(splits[13], 71), 0),
        "prompt_cache": draw_prompt_cache(jax.random.fold_in(splits[13], 71), 0),
        "suffix_table": jax.vmap(lambda own: jax.random.permutation(own, POOL_DEV))(jax.random.split(splits[9], N_REQ)).reshape((N_REQ, POOL_DEV)).astype(jnp.int32),
        "prompt_owner": jax.random.permutation(splits[10], PROMPT_PAGES).astype(jnp.int32),
        "suffix_len": uneven(splits[11], REQS, REQS * PAGE, SPAGES * PAGE, 2).astype(jnp.int32),
        "group_id": jnp.searchsorted(jnp.cumsum(uneven(splits[12], NGROUPS, REQS, 16, 1)), jnp.arange(REQS), side="right").astype(jnp.int32),
    }


def root_norm(values, gains):
    factor = lax.rsqrt(lax.optimization_barrier(jnp.mean(values * values, axis=-1, keepdims=True)) + 1e-06)
    return values * factor * gains

def reference(tokens, w_qkv, w_out, w_up, w_down, gain_attn, gain_mlp, suffix_cache, prompt_cache, suffix_table, prompt_owner, suffix_len, group_id):
    width = H * HD
    scale = 1.0 / HD ** 0.5
    span = SPAGES * PAGE
    offsets = (jnp.arange(N_REQ, dtype=jnp.int32) * POOL_DEV)[:, None, None]
    request_pages = (suffix_table.reshape(N_REQ, REQ_DEV, SPAGES).astype(jnp.int32) + offsets).reshape(REQS, SPAGES).astype(jnp.int32)
    group_pages = jnp.argsort(prompt_owner).astype(jnp.int32).reshape(NGROUPS, PPAGES)
    residual = tokens.astype(jnp.float32)
    new_keys = []
    new_vals = []
    for layer in range(L):
        normed = root_norm(residual, gain_attn[layer]).astype(jnp.bfloat16)
        projected = jnp.dot(normed, w_qkv[layer].reshape(3 * width, D).T, preferred_element_type=jnp.float32)
        projected = projected.reshape(REQS, 3, width).astype(jnp.bfloat16)
        query = projected[:, 0]
        key_new = projected[:, 1]
        val_new = projected[:, 2]
        new_keys.append(key_new)
        new_vals.append(val_new)
        suffix_keys = suffix_cache[layer, 0]
        suffix_vals = suffix_cache[layer, 1]
        prompt_keys = prompt_cache[layer, 0]
        prompt_vals = prompt_cache[layer, 1]

        def attend_one(item):
            query_row, key_row, val_row, pages, length, group = item
            chosen = group_pages[group]
            keys = jnp.concatenate([prompt_keys[chosen].transpose(0, 2, 1).reshape(-1, width), suffix_keys[pages].transpose(0, 2, 1).reshape(-1, width), key_row[None]], axis=0)
            vals = jnp.concatenate([prompt_vals[chosen].transpose(0, 2, 1).reshape(-1, width), suffix_vals[pages].transpose(0, 2, 1).reshape(-1, width), val_row[None]], axis=0)
            valid = jnp.concatenate([jnp.ones((PPAGES * PAGE,), dtype=bool), jnp.arange(span, dtype=jnp.int32) < length, jnp.ones((1,), dtype=bool)])
            query_heads = query_row.astype(jnp.float32).reshape(H, HD)
            key_heads = keys.astype(jnp.float32).reshape(-1, H, HD)
            val_heads = vals.astype(jnp.float32).reshape(-1, H, HD)
            scores = jnp.einsum('hd,thd->ht', query_heads, key_heads) * scale
            masked = jnp.where(valid[None, :], scores, -1e+30)
            top = lax.optimization_barrier(jnp.max(masked, axis=1, keepdims=True))
            weights = jnp.where(valid[None, :], jnp.exp(masked - top), 0.0)
            total = lax.optimization_barrier(jnp.sum(weights, axis=1))
            rounded = lax.optimization_barrier(weights.astype(jnp.bfloat16)).astype(jnp.float32)
            mixed = jnp.einsum('ht,thd->hd', rounded, val_heads) / total[:, None]
            return mixed.reshape(width).astype(jnp.bfloat16)
        attended = lax.map(attend_one, (query, key_new, val_new, request_pages, suffix_len, group_id))
        residual = residual + jnp.dot(attended, w_out[layer], preferred_element_type=jnp.float32)
        normed = root_norm(residual, gain_mlp[layer]).astype(jnp.bfloat16)
        hidden_units = jax.nn.silu(jnp.dot(normed, w_up[layer].T, preferred_element_type=jnp.float32)).astype(jnp.bfloat16)
        residual = residual + jnp.dot(hidden_units, w_down[layer], preferred_element_type=jnp.float32)
    new_cache = jnp.stack([jnp.stack(new_keys), jnp.stack(new_vals)], axis=1)
    return (residual.astype(jnp.bfloat16), new_cache)
```

```python
import math

import jax
import jax.numpy as jnp
from jax import lax
from jax.sharding import PartitionSpec as P

HD = 80
PPAGES = 4


NEG_FLOOR = -1e30


def root_norm(values, gains):
    factor = lax.rsqrt(jnp.mean(values * values, axis=-1, keepdims=True) + 1e-06)
    return values * factor * gains


def head_sum(value, count):
    step = 1
    while step < count:
        pairs = [(i, i ^ step) for i in range(count)]
        value = value + lax.ppermute(value, "head", pairs)
        step *= 2
    return value


def ring_gather(value, count):
    outs = [value]
    for shift in range(1, count):
        pairs = [(i, (i + shift) % count) for i in range(count)]
        outs.append(lax.ppermute(value, "req", pairs))
    return jnp.stack(outs)


def ring_return(parts, count):
    outs = [parts[0]]
    for shift in range(1, count):
        pairs = [(i, (i - shift) % count) for i in range(count)]
        outs.append(lax.ppermute(parts[shift], "req", pairs))
    return jnp.stack(outs)


def softmax_part(scores, mask, values_fn, axes):
    top = jnp.max(jnp.where(mask, scores, NEG_FLOOR), axis=axes)
    expand = top.reshape(top.shape + (1,) * len(axes))
    weights = jnp.exp(jnp.where(mask, scores - expand, NEG_FLOOR))
    total = jnp.sum(weights, axis=axes)
    mixed = values_fn(weights.astype(jnp.bfloat16))
    return top, total, mixed


def attend(query, key_new, val_new, layer_suffix, layer_prompt, valid, page_group, group_all, n_req):
    row_count = query.shape[0]
    head_count = query.shape[1] // HD
    scale = 1.0 / math.sqrt(HD)
    page_len = layer_suffix.shape[3]
    query_heads = query.reshape(row_count, head_count, HD)
    key_heads = key_new.reshape(row_count, head_count, HD)
    val_heads = val_new.reshape(row_count, head_count, HD)

    query_all = ring_gather(query_heads, n_req)

    pool = layer_suffix.shape[1]
    s_keys = layer_suffix[0].reshape(pool, head_count, HD, page_len)
    s_vals = layer_suffix[1].reshape(pool, head_count, HD, page_len)
    s_scores = (
        jnp.einsum("ihd,phdt->ihpt", query_heads, s_keys, preferred_element_type=jnp.float32)
        * scale
    )
    s_top, s_total, s_mixed = softmax_part(
        s_scores,
        valid[:, None],
        lambda w: jnp.einsum("ihpt,phdt->ihd", w, s_vals, preferred_element_type=jnp.float32),
        (2, 3),
    )
    own = (
        jnp.einsum("rhd,rhd->rh", query_heads, key_heads, preferred_element_type=jnp.float32)
        * scale
    )

    count = layer_prompt.shape[1]
    p_keys = layer_prompt[0].reshape(count, head_count, HD, page_len)
    p_vals = layer_prompt[1].reshape(count, head_count, HD, page_len)
    p_scores = (
        jnp.einsum("sihd,khdt->sihkt", query_all, p_keys, preferred_element_type=jnp.float32)
        * scale
    )
    match = (group_all[:, :, None] == page_group[None, None, :])[:, :, None, :, None]
    p_top, p_total, p_mixed = softmax_part(
        p_scores,
        match,
        lambda w: jnp.einsum("sihkt,khdt->sihd", w, p_vals, preferred_element_type=jnp.float32),
        (3, 4),
    )
    packed = jnp.concatenate([p_mixed, p_top[..., None], p_total[..., None]], axis=-1)
    back = ring_return(packed, n_req)
    b_mixed = back[..., :HD]
    b_top = back[..., HD]
    b_total = back[..., HD + 1]

    top = jnp.maximum(jnp.maximum(s_top, own), jnp.max(b_top, axis=0))
    s_factor = jnp.exp(s_top - top)
    b_factor = jnp.exp(b_top - top[None])
    own_weight = jnp.exp(own - top)
    total = s_total * s_factor + jnp.sum(b_total * b_factor, axis=0) + own_weight
    mixed = (
        s_mixed * s_factor[..., None]
        + jnp.sum(b_mixed * b_factor[..., None], axis=0)
        + own_weight.astype(jnp.bfloat16).astype(jnp.float32)[..., None]
        * val_heads.astype(jnp.float32)
    )
    return (mixed / total[..., None]).reshape(row_count, -1).astype(jnp.bfloat16)


def make_local(n_req, n_head):
    def local(
        tokens,
        w_qkv,
        w_out,
        w_up,
        w_down,
        gain_attn,
        gain_mlp,
        suffix_cache,
        prompt_cache,
        suffix_table,
        prompt_owner,
        suffix_len,
        group_id,
    ):
        row_count = tokens.shape[0]
        layer_count = w_qkv.shape[0]
        width_here = w_qkv.shape[2]
        model_width = w_qkv.shape[3]
        page_len = suffix_cache.shape[4]
        pool = suffix_cache.shape[2]
        own_pages = suffix_table.shape[1] // row_count
        prompt_here = prompt_cache.shape[2]

        table = suffix_table[0].reshape(row_count, own_pages)
        rows = jnp.arange(page_len, dtype=jnp.int32)
        page_ids = jnp.arange(pool, dtype=jnp.int32)
        valid = jnp.zeros((row_count, pool, page_len), dtype=bool)
        for slot in range(own_pages):
            chosen = (table[:, slot][:, None] == page_ids[None, :])[:, :, None]
            filled = (slot * page_len + rows)[None, None, :] < suffix_len[:, None, None]
            valid = valid | (chosen & filled)

        here = lax.axis_index("req")
        page_group = lax.dynamic_slice(prompt_owner, (here * prompt_here,), (prompt_here,)) // PPAGES
        group_all = ring_gather(group_id, n_req)

        whole = tokens.astype(jnp.float32)
        normed = root_norm(whole, gain_attn[0]).astype(jnp.bfloat16)
        residual = whole
        new_keys = []
        new_vals = []
        for layer in range(layer_count):
            projected = jnp.einsum(
                "rd,kd->rk",
                normed,
                w_qkv[layer].reshape(3 * width_here, model_width),
                preferred_element_type=jnp.float32,
            )
            projected = projected.reshape(row_count, 3, width_here).astype(jnp.bfloat16)
            query = projected[:, 0]
            key_new = projected[:, 1]
            val_new = projected[:, 2]
            new_keys.append(key_new)
            new_vals.append(val_new)
            attended = attend(
                query,
                key_new,
                val_new,
                suffix_cache[layer],
                prompt_cache[layer],
                valid,
                page_group,
                group_all,
                n_req,
            )
            partial_value = jnp.dot(attended, w_out[layer], preferred_element_type=jnp.float32)
            residual = residual + head_sum(partial_value, n_head)
            normed = root_norm(residual, gain_mlp[layer]).astype(jnp.bfloat16)
            hidden_units = jax.nn.silu(
                jnp.einsum("rd,fd->rf", normed, w_up[layer], preferred_element_type=jnp.float32)
            ).astype(jnp.bfloat16)
            partial_value = jnp.dot(hidden_units, w_down[layer], preferred_element_type=jnp.float32)
            residual = residual + head_sum(partial_value, n_head)
            if layer + 1 < layer_count:
                normed = root_norm(residual, gain_attn[layer + 1]).astype(jnp.bfloat16)
        hidden = residual.astype(jnp.bfloat16)
        new_cache = jnp.stack([jnp.stack(new_keys), jnp.stack(new_vals)], axis=1)
        return (hidden, new_cache)

    return local


def solution(mesh):
    placed = (
        P("req", None),
        P(None, None, "head", None),
        P(None, "head", None),
        P(None, "head", None),
        P(None, "head", None),
        P(),
        P(),
        P(None, None, "req", "head", None),
        P(None, None, "req", "head", None),
        P("req", None),
        P(),
        P("req"),
        P("req"),
    )
    return jax.shard_map(
        make_local(mesh.shape["req"], mesh.shape["head"]),
        mesh=mesh,
        in_specs=placed,
        out_specs=(P("req", None), P(None, None, "req", "head")),
        check_vma=False,
    )
```

```python
import math

import jax
import jax.numpy as jnp
from jax import lax
from jax.sharding import PartitionSpec as P

HD = 80
PPAGES = 4


NEG_FLOOR = -1e30


def root_norm(values, gains):
    factor = lax.rsqrt(jnp.mean(values * values, axis=-1, keepdims=True) + 1e-06)
    return values * factor * gains


def head_sum(value, count):
    step = 1
    while step < count:
        pairs = [(i, i ^ step) for i in range(count)]
        value = value + lax.ppermute(value, "head", pairs)
        step *= 2
    return value


def spread(value, count):
    copies = jnp.broadcast_to(value[None], (count,) + value.shape)
    return lax.all_to_all(copies, "req", 0, 0, tiled=True)


def send_home(parts, count):
    return lax.all_to_all(parts, "req", 0, 0, tiled=True)


def softmax_part(scores, mask, values_fn, axes):
    top = jnp.max(jnp.where(mask, scores, NEG_FLOOR), axis=axes)
    expand = top.reshape(top.shape + (1,) * len(axes))
    weights = jnp.exp(jnp.where(mask, scores - expand, NEG_FLOOR))
    total = jnp.sum(weights, axis=axes)
    mixed = values_fn(weights.astype(jnp.bfloat16))
    return top, total, mixed


def attend(query_all, query, key_new, val_new, layer_suffix, layer_prompt, valid, page_group, group_all, n_req):
    row_count = query.shape[0]
    head_count = query.shape[1] // HD
    scale = 1.0 / math.sqrt(HD)
    page_len = layer_suffix.shape[3]
    query_heads = query.reshape(row_count, head_count, HD)
    key_heads = key_new.reshape(row_count, head_count, HD)
    val_heads = val_new.reshape(row_count, head_count, HD)

    pool = layer_suffix.shape[1]
    s_keys = layer_suffix[0].reshape(pool, head_count, HD, page_len)
    s_vals = layer_suffix[1].reshape(pool, head_count, HD, page_len)
    s_scores = (
        jnp.einsum("ihd,phdt->ihpt", query_heads, s_keys, preferred_element_type=jnp.float32)
        * scale
    )
    s_top, s_total, s_mixed = softmax_part(
        s_scores,
        valid[:, None],
        lambda w: jnp.einsum("ihpt,phdt->ihd", w, s_vals, preferred_element_type=jnp.float32),
        (2, 3),
    )
    own = (
        jnp.einsum("rhd,rhd->rh", query_heads, key_heads, preferred_element_type=jnp.float32)
        * scale
    )

    count = layer_prompt.shape[1]
    p_keys = layer_prompt[0].reshape(count, head_count, HD, page_len)
    p_vals = layer_prompt[1].reshape(count, head_count, HD, page_len)
    p_scores = (
        jnp.einsum("sihd,khdt->sihkt", query_all, p_keys, preferred_element_type=jnp.float32)
        * scale
    )
    match = (group_all[:, :, None] == page_group[None, None, :])[:, :, None, :, None]
    p_top, p_total, p_mixed = softmax_part(
        p_scores,
        match,
        lambda w: jnp.einsum("sihkt,khdt->sihd", w, p_vals, preferred_element_type=jnp.float32),
        (3, 4),
    )
    packed = jnp.concatenate([p_mixed, p_top[..., None], p_total[..., None]], axis=-1)
    back = send_home(packed, n_req)
    b_mixed = back[..., :HD]
    b_top = back[..., HD]
    b_total = back[..., HD + 1]

    top = jnp.maximum(jnp.maximum(s_top, own), jnp.max(b_top, axis=0))
    s_factor = jnp.exp(s_top - top)
    b_factor = jnp.exp(b_top - top[None])
    own_weight = jnp.exp(own - top)
    total = s_total * s_factor + jnp.sum(b_total * b_factor, axis=0) + own_weight
    mixed = (
        s_mixed * s_factor[..., None]
        + jnp.sum(b_mixed * b_factor[..., None], axis=0)
        + own_weight.astype(jnp.bfloat16).astype(jnp.float32)[..., None]
        * val_heads.astype(jnp.float32)
    )
    return (mixed / total[..., None]).reshape(row_count, -1).astype(jnp.bfloat16)


def make_local(n_req, n_head):
    def local(
        tokens,
        w_qkv,
        w_out,
        w_up,
        w_down,
        gain_attn,
        gain_mlp,
        suffix_cache,
        prompt_cache,
        suffix_table,
        prompt_owner,
        suffix_len,
        group_id,
    ):
        row_count = tokens.shape[0]
        layer_count = w_qkv.shape[0]
        width_here = w_qkv.shape[2]
        model_width = w_qkv.shape[3]
        page_len = suffix_cache.shape[4]
        pool = suffix_cache.shape[2]
        own_pages = suffix_table.shape[1] // row_count
        prompt_here = prompt_cache.shape[2]

        table = suffix_table[0].reshape(row_count, own_pages)
        rows = jnp.arange(page_len, dtype=jnp.int32)
        page_ids = jnp.arange(pool, dtype=jnp.int32)
        valid = jnp.zeros((row_count, pool, page_len), dtype=bool)
        for slot in range(own_pages):
            chosen = (table[:, slot][:, None] == page_ids[None, :])[:, :, None]
            filled = (slot * page_len + rows)[None, None, :] < suffix_len[:, None, None]
            valid = valid | (chosen & filled)

        here = lax.axis_index("req")
        page_group = lax.dynamic_slice(prompt_owner, (here * prompt_here,), (prompt_here,)) // PPAGES

        whole = tokens.astype(jnp.float32)
        normed = root_norm(whole, gain_attn[0]).astype(jnp.bfloat16)
        residual = whole
        new_keys = []
        new_vals = []
        for layer in range(layer_count):
            projected = jnp.einsum(
                "rd,kd->rk",
                normed,
                w_qkv[layer].reshape(3 * width_here, model_width),
                preferred_element_type=jnp.float32,
            )
            projected = projected.reshape(row_count, 3, width_here).astype(jnp.bfloat16)
            query = projected[:, 0]
            key_new = projected[:, 1]
            val_new = projected[:, 2]
            new_keys.append(key_new)
            new_vals.append(val_new)
            if layer == 0:
                payload = jnp.concatenate([query, group_id.astype(jnp.bfloat16)[:, None]], axis=1)
                gathered = spread(payload, n_req)
                group_all = gathered[:, :, width_here].astype(jnp.int32)
            else:
                gathered = spread(query, n_req)
            query_all = gathered[:, :, :width_here].reshape(n_req, row_count, -1, HD)
            attended = attend(
                query_all,
                query,
                key_new,
                val_new,
                suffix_cache[layer],
                prompt_cache[layer],
                valid,
                page_group,
                group_all,
                n_req,
            )
            partial_value = jnp.dot(attended, w_out[layer], preferred_element_type=jnp.float32)
            residual = residual + head_sum(partial_value, n_head)
            normed = root_norm(residual, gain_mlp[layer]).astype(jnp.bfloat16)
            hidden_units = jax.nn.silu(
                jnp.einsum("rd,fd->rf", normed, w_up[layer], preferred_element_type=jnp.float32)
            ).astype(jnp.bfloat16)
            partial_value = jnp.dot(hidden_units, w_down[layer], preferred_element_type=jnp.float32)
            residual = residual + head_sum(partial_value, n_head)
            if layer + 1 < layer_count:
                normed = root_norm(residual, gain_attn[layer + 1]).astype(jnp.bfloat16)
        hidden = residual.astype(jnp.bfloat16)
        new_cache = jnp.stack([jnp.stack(new_keys), jnp.stack(new_vals)], axis=1)
        return (hidden, new_cache)

    return local


def solution(mesh):
    placed = (
        P("req", None),
        P(None, None, "head", None),
        P(None, "head", None),
        P(None, "head", None),
        P(None, "head", None),
        P(),
        P(),
        P(None, None, "req", "head", None),
        P(None, None, "req", "head", None),
        P("req", None),
        P(),
        P("req"),
        P("req"),
    )
    return jax.shard_map(
        make_local(mesh.shape["req"], mesh.shape["head"]),
        mesh=mesh,
        in_specs=placed,
        out_specs=(P("req", None), P(None, None, "req", "head")),
        check_vma=False,
    )
```

```python
import math

import jax
import jax.numpy as jnp
from jax import lax
from jax.sharding import PartitionSpec as P

HD = 80
PPAGES = 4


NEG_FLOOR = -1e30


def root_norm(values, gains):
    factor = lax.rsqrt(jnp.mean(values * values, axis=-1, keepdims=True) + 1e-06)
    return values * factor * gains


def head_sum(value, count):
    chips = count // 2
    partners = [
        [i ^ 1 for i in range(count)],
        [i ^ 2 for i in range(count)],
        [(chips - 1 - i // 2) * 2 + i % 2 for i in range(count)],
    ]
    for partner in partners:
        value = value + lax.ppermute(value, "head", [(i, partner[i]) for i in range(count)])
    return value


def spread(value, count):
    copies = jnp.broadcast_to(value[None], (count,) + value.shape)
    return lax.all_to_all(copies, "req", 0, 0, tiled=True)


def send_home(parts, count):
    return lax.all_to_all(parts, "req", 0, 0, tiled=True)


def softmax_part(scores, mask, values_fn, axes):
    top = jnp.max(jnp.where(mask, scores, NEG_FLOOR), axis=axes)
    expand = top.reshape(top.shape + (1,) * len(axes))
    weights = jnp.exp(jnp.where(mask, scores - expand, NEG_FLOOR))
    total = jnp.sum(weights, axis=axes)
    mixed = values_fn(weights.astype(jnp.bfloat16))
    return top, total, mixed


def attend(query_all, query, key_new, val_new, layer_suffix, layer_prompt, valid, page_group, group_all, n_req):
    row_count = query.shape[0]
    head_count = query.shape[1] // HD
    scale = 1.0 / math.sqrt(HD)
    page_len = layer_suffix.shape[3]
    query_heads = query.reshape(row_count, head_count, HD)
    key_heads = key_new.reshape(row_count, head_count, HD)
    val_heads = val_new.reshape(row_count, head_count, HD)

    pool = layer_suffix.shape[1]
    s_keys = layer_suffix[0].reshape(pool, head_count, HD, page_len)
    s_vals = layer_suffix[1].reshape(pool, head_count, HD, page_len)
    s_scores = (
        jnp.einsum("ihd,phdt->ihpt", query_heads, s_keys, preferred_element_type=jnp.float32)
        * scale
    )
    s_top, s_total, s_mixed = softmax_part(
        s_scores,
        valid[:, None],
        lambda w: jnp.einsum("ihpt,phdt->ihd", w, s_vals, preferred_element_type=jnp.float32),
        (2, 3),
    )
    own = (
        jnp.einsum("rhd,rhd->rh", query_heads, key_heads, preferred_element_type=jnp.float32)
        * scale
    )

    count = layer_prompt.shape[1]
    p_keys = layer_prompt[0].reshape(count, head_count, HD, page_len)
    p_vals = layer_prompt[1].reshape(count, head_count, HD, page_len)
    p_scores = (
        jnp.einsum("sihd,khdt->sihkt", query_all, p_keys, preferred_element_type=jnp.float32)
        * scale
    )
    match = (group_all[:, :, None] == page_group[None, None, :])[:, :, None, :, None]
    p_top, p_total, p_mixed = softmax_part(
        p_scores,
        match,
        lambda w: jnp.einsum("sihkt,khdt->sihd", w, p_vals, preferred_element_type=jnp.float32),
        (3, 4),
    )
    packed = jnp.concatenate([p_mixed, p_top[..., None], p_total[..., None]], axis=-1)
    back = send_home(packed, n_req)
    b_mixed = back[..., :HD]
    b_top = back[..., HD]
    b_total = back[..., HD + 1]

    top = jnp.maximum(jnp.maximum(s_top, own), jnp.max(b_top, axis=0))
    s_factor = jnp.exp(s_top - top)
    b_factor = jnp.exp(b_top - top[None])
    own_weight = jnp.exp(own - top)
    total = s_total * s_factor + jnp.sum(b_total * b_factor, axis=0) + own_weight
    mixed = (
        s_mixed * s_factor[..., None]
        + jnp.sum(b_mixed * b_factor[..., None], axis=0)
        + own_weight.astype(jnp.bfloat16).astype(jnp.float32)[..., None]
        * val_heads.astype(jnp.float32)
    )
    return (mixed / total[..., None]).reshape(row_count, -1).astype(jnp.bfloat16)


def make_local(n_req, n_head):
    def local(
        tokens,
        w_qkv,
        w_out,
        w_up,
        w_down,
        gain_attn,
        gain_mlp,
        suffix_cache,
        prompt_cache,
        suffix_table,
        prompt_owner,
        suffix_len,
        group_id,
    ):
        row_count = tokens.shape[0]
        layer_count = w_qkv.shape[0]
        width_here = w_qkv.shape[2]
        model_width = w_qkv.shape[3]
        page_len = suffix_cache.shape[4]
        pool = suffix_cache.shape[2]
        own_pages = suffix_table.shape[1] // row_count
        prompt_here = prompt_cache.shape[2]

        table = suffix_table[0].reshape(row_count, own_pages)
        rows = jnp.arange(page_len, dtype=jnp.int32)
        page_ids = jnp.arange(pool, dtype=jnp.int32)
        valid = jnp.zeros((row_count, pool, page_len), dtype=bool)
        for slot in range(own_pages):
            chosen = (table[:, slot][:, None] == page_ids[None, :])[:, :, None]
            filled = (slot * page_len + rows)[None, None, :] < suffix_len[:, None, None]
            valid = valid | (chosen & filled)

        here = lax.axis_index("req")
        page_group = lax.dynamic_slice(prompt_owner, (here * prompt_here,), (prompt_here,)) // PPAGES

        whole = tokens.astype(jnp.float32)
        normed = root_norm(whole, gain_attn[0]).astype(jnp.bfloat16)
        residual = whole
        new_keys = []
        new_vals = []
        for layer in range(layer_count):
            projected = jnp.einsum(
                "rd,kd->rk",
                normed,
                w_qkv[layer].reshape(3 * width_here, model_width),
                preferred_element_type=jnp.float32,
            )
            projected = projected.reshape(row_count, 3, width_here).astype(jnp.bfloat16)
            query = projected[:, 0]
            key_new = projected[:, 1]
            val_new = projected[:, 2]
            new_keys.append(key_new)
            new_vals.append(val_new)
            if layer == 0:
                payload = jnp.concatenate([query, group_id.astype(jnp.bfloat16)[:, None]], axis=1)
                gathered = spread(payload, n_req)
                group_all = gathered[:, :, width_here].astype(jnp.int32)
            else:
                gathered = spread(query, n_req)
            query_all = gathered[:, :, :width_here].reshape(n_req, row_count, -1, HD)
            attended = attend(
                query_all,
                query,
                key_new,
                val_new,
                suffix_cache[layer],
                prompt_cache[layer],
                valid,
                page_group,
                group_all,
                n_req,
            )
            partial_value = jnp.dot(attended, w_out[layer], preferred_element_type=jnp.float32)
            residual = residual + head_sum(partial_value, n_head)
            normed = root_norm(residual, gain_mlp[layer]).astype(jnp.bfloat16)
            hidden_units = jax.nn.silu(
                jnp.einsum("rd,fd->rf", normed, w_up[layer], preferred_element_type=jnp.float32)
            ).astype(jnp.bfloat16)
            partial_value = jnp.dot(hidden_units, w_down[layer], preferred_element_type=jnp.float32)
            residual = residual + head_sum(partial_value, n_head)
            if layer + 1 < layer_count:
                normed = root_norm(residual, gain_attn[layer + 1]).astype(jnp.bfloat16)
        hidden = residual.astype(jnp.bfloat16)
        new_cache = jnp.stack([jnp.stack(new_keys), jnp.stack(new_vals)], axis=1)
        return (hidden, new_cache)

    return local


def solution(mesh):
    placed = (
        P("req", None),
        P(None, None, "head", None),
        P(None, "head", None),
        P(None, "head", None),
        P(None, "head", None),
        P(),
        P(),
        P(None, None, "req", "head", None),
        P(None, None, "req", "head", None),
        P("req", None),
        P(),
        P("req"),
        P("req"),
    )
    return jax.shard_map(
        make_local(mesh.shape["req"], mesh.shape["head"]),
        mesh=mesh,
        in_specs=placed,
        out_specs=(P("req", None), P(None, None, "req", "head")),
        check_vma=False,
    )
```

```python
import math

import jax
import jax.numpy as jnp
from jax import lax
from jax.sharding import PartitionSpec as P

HD = 80
PPAGES = 4


NEG_FLOOR = -1e30


def root_norm(values, gains):
    factor = lax.rsqrt(jnp.mean(values * values, axis=-1, keepdims=True) + 1e-06)
    return values * factor * gains


def head_sum(value, count):
    chips = count // 2
    partners = [
        [i ^ 1 for i in range(count)],
        [i ^ 2 for i in range(count)],
        [(chips - 1 - i // 2) * 2 + i % 2 for i in range(count)],
    ]
    for partner in partners:
        value = value + lax.ppermute(value, "head", [(i, partner[i]) for i in range(count)])
    return value


def spread(value, count):
    copies = jnp.broadcast_to(value[None], (count,) + value.shape)
    return lax.all_to_all(copies, "req", 0, 0, tiled=True)


def send_home(parts, count):
    return lax.all_to_all(parts, "req", 0, 0, tiled=True)


def softmax_part(scores, mask, values_fn, axes, coarse=False):
    top = jnp.max(jnp.where(mask, scores, NEG_FLOOR), axis=axes)
    if coarse:
        top = top.astype(jnp.bfloat16).astype(jnp.float32)
    expand = top.reshape(top.shape + (1,) * len(axes))
    weights = jnp.exp(jnp.where(mask, scores - expand, NEG_FLOOR))
    total = jnp.sum(weights, axis=axes)
    mixed = values_fn(weights.astype(jnp.bfloat16))
    return top, total, mixed


def attend(query_all, query, key_new, val_new, layer_suffix, layer_prompt, valid, page_group, group_all, n_req):
    row_count = query.shape[0]
    head_count = query.shape[1] // HD
    scale = 1.0 / math.sqrt(HD)
    page_len = layer_suffix.shape[3]
    query_heads = query.reshape(row_count, head_count, HD)
    key_heads = key_new.reshape(row_count, head_count, HD)
    val_heads = val_new.reshape(row_count, head_count, HD)

    pool = layer_suffix.shape[1]
    s_keys = layer_suffix[0].reshape(pool, head_count, HD, page_len)
    s_vals = layer_suffix[1].reshape(pool, head_count, HD, page_len)
    s_scores = (
        jnp.einsum("ihd,phdt->ihpt", query_heads, s_keys, preferred_element_type=jnp.float32)
        * scale
    )
    s_top, s_total, s_mixed = softmax_part(
        s_scores,
        valid[:, None],
        lambda w: jnp.einsum("ihpt,phdt->ihd", w, s_vals, preferred_element_type=jnp.float32),
        (2, 3),
    )
    own = (
        jnp.einsum("rhd,rhd->rh", query_heads, key_heads, preferred_element_type=jnp.float32)
        * scale
    )

    count = layer_prompt.shape[1]
    p_keys = layer_prompt[0].reshape(count, head_count, HD, page_len)
    p_vals = layer_prompt[1].reshape(count, head_count, HD, page_len)
    p_scores = (
        jnp.einsum("sihd,khdt->sihkt", query_all, p_keys, preferred_element_type=jnp.float32)
        * scale
    )
    match = (group_all[:, :, None] == page_group[None, None, :])[:, :, None, :, None]
    p_top, p_total, p_mixed = softmax_part(
        p_scores,
        match,
        lambda w: jnp.einsum("sihkt,khdt->sihd", w, p_vals, preferred_element_type=jnp.float32),
        (3, 4),
        coarse=True,
    )
    total_high = p_total.astype(jnp.bfloat16)
    total_low = (p_total - total_high.astype(jnp.float32)).astype(jnp.bfloat16)
    packed = jnp.concatenate(
        [
            p_mixed.astype(jnp.bfloat16),
            p_top.astype(jnp.bfloat16)[..., None],
            total_high[..., None],
            total_low[..., None],
        ],
        axis=-1,
    )
    back = send_home(packed, n_req)
    b_mixed = back[..., :HD].astype(jnp.float32)
    b_top = back[..., HD].astype(jnp.float32)
    b_total = back[..., HD + 1].astype(jnp.float32) + back[..., HD + 2].astype(jnp.float32)

    top = jnp.maximum(jnp.maximum(s_top, own), jnp.max(b_top, axis=0))
    s_factor = jnp.exp(s_top - top)
    b_factor = jnp.exp(b_top - top[None])
    own_weight = jnp.exp(own - top)
    total = s_total * s_factor + jnp.sum(b_total * b_factor, axis=0) + own_weight
    mixed = (
        s_mixed * s_factor[..., None]
        + jnp.sum(b_mixed * b_factor[..., None], axis=0)
        + own_weight.astype(jnp.bfloat16).astype(jnp.float32)[..., None]
        * val_heads.astype(jnp.float32)
    )
    return (mixed / total[..., None]).reshape(row_count, -1).astype(jnp.bfloat16)


def make_local(n_req, n_head):
    def local(
        tokens,
        w_qkv,
        w_out,
        w_up,
        w_down,
        gain_attn,
        gain_mlp,
        suffix_cache,
        prompt_cache,
        suffix_table,
        prompt_owner,
        suffix_len,
        group_id,
    ):
        row_count = tokens.shape[0]
        layer_count = w_qkv.shape[0]
        width_here = w_qkv.shape[2]
        model_width = w_qkv.shape[3]
        page_len = suffix_cache.shape[4]
        pool = suffix_cache.shape[2]
        own_pages = suffix_table.shape[1] // row_count
        prompt_here = prompt_cache.shape[2]

        table = suffix_table[0].reshape(row_count, own_pages)
        rows = jnp.arange(page_len, dtype=jnp.int32)
        page_ids = jnp.arange(pool, dtype=jnp.int32)
        valid = jnp.zeros((row_count, pool, page_len), dtype=bool)
        for slot in range(own_pages):
            chosen = (table[:, slot][:, None] == page_ids[None, :])[:, :, None]
            filled = (slot * page_len + rows)[None, None, :] < suffix_len[:, None, None]
            valid = valid | (chosen & filled)

        here = lax.axis_index("req")
        page_group = lax.dynamic_slice(prompt_owner, (here * prompt_here,), (prompt_here,)) // PPAGES

        whole = tokens.astype(jnp.float32)
        normed = root_norm(whole, gain_attn[0]).astype(jnp.bfloat16)
        residual = whole
        new_keys = []
        new_vals = []
        for layer in range(layer_count):
            projected = jnp.einsum(
                "rd,kd->rk",
                normed,
                w_qkv[layer].reshape(3 * width_here, model_width),
                preferred_element_type=jnp.float32,
            )
            projected = projected.reshape(row_count, 3, width_here).astype(jnp.bfloat16)
            query = projected[:, 0]
            key_new = projected[:, 1]
            val_new = projected[:, 2]
            new_keys.append(key_new)
            new_vals.append(val_new)
            if layer == 0:
                payload = jnp.concatenate([query, group_id.astype(jnp.bfloat16)[:, None]], axis=1)
                gathered = spread(payload, n_req)
                group_all = gathered[:, :, width_here].astype(jnp.int32)
            else:
                gathered = spread(query, n_req)
            query_all = gathered[:, :, :width_here].reshape(n_req, row_count, -1, HD)
            attended = attend(
                query_all,
                query,
                key_new,
                val_new,
                suffix_cache[layer],
                prompt_cache[layer],
                valid,
                page_group,
                group_all,
                n_req,
            )
            partial_value = jnp.dot(attended, w_out[layer], preferred_element_type=jnp.float32)
            residual = residual + head_sum(partial_value, n_head)
            normed = root_norm(residual, gain_mlp[layer]).astype(jnp.bfloat16)
            hidden_units = jax.nn.silu(
                jnp.einsum("rd,fd->rf", normed, w_up[layer], preferred_element_type=jnp.float32)
            ).astype(jnp.bfloat16)
            partial_value = jnp.dot(hidden_units, w_down[layer], preferred_element_type=jnp.float32)
            residual = residual + head_sum(partial_value, n_head)
            if layer + 1 < layer_count:
                normed = root_norm(residual, gain_attn[layer + 1]).astype(jnp.bfloat16)
        hidden = residual.astype(jnp.bfloat16)
        new_cache = jnp.stack([jnp.stack(new_keys), jnp.stack(new_vals)], axis=1)
        return (hidden, new_cache)

    return local


def solution(mesh):
    placed = (
        P("req", None),
        P(None, None, "head", None),
        P(None, "head", None),
        P(None, "head", None),
        P(None, "head", None),
        P(),
        P(),
        P(None, None, "req", "head", None),
        P(None, None, "req", "head", None),
        P("req", None),
        P(),
        P("req"),
        P("req"),
    )
    return jax.shard_map(
        make_local(mesh.shape["req"], mesh.shape["head"]),
        mesh=mesh,
        in_specs=placed,
        out_specs=(P("req", None), P(None, None, "req", "head")),
        check_vma=False,
    )
```

```python
import math

import jax
import jax.numpy as jnp
from jax import lax
from jax.sharding import PartitionSpec as P

HD = 80
PPAGES = 4


NEG_FLOOR = -1e30


def root_norm(values, gains):
    factor = lax.rsqrt(jnp.mean(values * values, axis=-1, keepdims=True) + 1e-06)
    return values * factor * gains


def head_sum(value, count):
    chips = count // 2
    value = value + lax.ppermute(value, "head", [(i, i ^ 1) for i in range(count)])

    def from_chip(shift):
        pairs = [(i, ((i // 2 + shift) % chips) * 2 + i % 2) for i in range(count)]
        return lax.ppermute(value, "head", pairs)

    later = from_chip(1)
    opposite = from_chip(2)
    earlier = from_chip(chips - 1)
    return (value + opposite) + (later + earlier)


def spread(value, count):
    copies = jnp.broadcast_to(value[None], (count,) + value.shape)
    return lax.all_to_all(copies, "req", 0, 0, tiled=True)


def send_home(parts, count):
    return lax.all_to_all(parts, "req", 0, 0, tiled=True)


def softmax_part(scores, mask, values_fn, axes):
    top = jnp.max(jnp.where(mask, scores, NEG_FLOOR), axis=axes)
    expand = top.reshape(top.shape + (1,) * len(axes))
    weights = jnp.exp(jnp.where(mask, scores - expand, NEG_FLOOR))
    total = jnp.sum(weights, axis=axes)
    mixed = values_fn(weights.astype(jnp.bfloat16))
    return top, total, mixed


def attend(query_all, query, key_new, val_new, layer_suffix, layer_prompt, valid, page_group, group_all, n_req):
    row_count = query.shape[0]
    head_count = query.shape[1] // HD
    scale = 1.0 / math.sqrt(HD)
    page_len = layer_suffix.shape[3]
    query_heads = query.reshape(row_count, head_count, HD)
    key_heads = key_new.reshape(row_count, head_count, HD)
    val_heads = val_new.reshape(row_count, head_count, HD)

    pool = layer_suffix.shape[1]
    s_keys = layer_suffix[0].reshape(pool, head_count, HD, page_len)
    s_vals = layer_suffix[1].reshape(pool, head_count, HD, page_len)
    s_scores = (
        jnp.einsum("ihd,phdt->ihpt", query_heads, s_keys, preferred_element_type=jnp.float32)
        * scale
    )
    s_top, s_total, s_mixed = softmax_part(
        s_scores,
        valid[:, None],
        lambda w: jnp.einsum("ihpt,phdt->ihd", w, s_vals, preferred_element_type=jnp.float32),
        (2, 3),
    )
    own = (
        jnp.einsum("rhd,rhd->rh", query_heads, key_heads, preferred_element_type=jnp.float32)
        * scale
    )

    count = layer_prompt.shape[1]
    p_keys = layer_prompt[0].reshape(count, head_count, HD, page_len)
    p_vals = layer_prompt[1].reshape(count, head_count, HD, page_len)
    p_scores = (
        jnp.einsum("sihd,khdt->sihkt", query_all, p_keys, preferred_element_type=jnp.float32)
        * scale
    )
    match = (group_all[:, :, None] == page_group[None, None, :])[:, :, None, :, None]
    p_top, p_total, p_mixed = softmax_part(
        p_scores,
        match,
        lambda w: jnp.einsum("sihkt,khdt->sihd", w, p_vals, preferred_element_type=jnp.float32),
        (3, 4),
    )
    packed = jnp.concatenate([p_mixed, p_top[..., None], p_total[..., None]], axis=-1)
    back = send_home(packed, n_req)
    b_mixed = back[..., :HD]
    b_top = back[..., HD]
    b_total = back[..., HD + 1]

    top = jnp.maximum(jnp.maximum(s_top, own), jnp.max(b_top, axis=0))
    s_factor = jnp.exp(s_top - top)
    b_factor = jnp.exp(b_top - top[None])
    own_weight = jnp.exp(own - top)
    total = s_total * s_factor + jnp.sum(b_total * b_factor, axis=0) + own_weight
    mixed = (
        s_mixed * s_factor[..., None]
        + jnp.sum(b_mixed * b_factor[..., None], axis=0)
        + own_weight.astype(jnp.bfloat16).astype(jnp.float32)[..., None]
        * val_heads.astype(jnp.float32)
    )
    return (mixed / total[..., None]).reshape(row_count, -1).astype(jnp.bfloat16)


def make_local(n_req, n_head):
    def local(
        tokens,
        w_qkv,
        w_out,
        w_up,
        w_down,
        gain_attn,
        gain_mlp,
        suffix_cache,
        prompt_cache,
        suffix_table,
        prompt_owner,
        suffix_len,
        group_id,
    ):
        row_count = tokens.shape[0]
        layer_count = w_qkv.shape[0]
        width_here = w_qkv.shape[2]
        model_width = w_qkv.shape[3]
        page_len = suffix_cache.shape[4]
        pool = suffix_cache.shape[2]
        own_pages = suffix_table.shape[1] // row_count
        prompt_here = prompt_cache.shape[2]

        table = suffix_table[0].reshape(row_count, own_pages)
        rows = jnp.arange(page_len, dtype=jnp.int32)
        page_ids = jnp.arange(pool, dtype=jnp.int32)
        valid = jnp.zeros((row_count, pool, page_len), dtype=bool)
        for slot in range(own_pages):
            chosen = (table[:, slot][:, None] == page_ids[None, :])[:, :, None]
            filled = (slot * page_len + rows)[None, None, :] < suffix_len[:, None, None]
            valid = valid | (chosen & filled)

        here = lax.axis_index("req")
        page_group = lax.dynamic_slice(prompt_owner, (here * prompt_here,), (prompt_here,)) // PPAGES

        whole = tokens.astype(jnp.float32)
        normed = root_norm(whole, gain_attn[0]).astype(jnp.bfloat16)
        residual = whole
        new_keys = []
        new_vals = []
        for layer in range(layer_count):
            projected = jnp.einsum(
                "rd,kd->rk",
                normed,
                w_qkv[layer].reshape(3 * width_here, model_width),
                preferred_element_type=jnp.float32,
            )
            projected = projected.reshape(row_count, 3, width_here).astype(jnp.bfloat16)
            query = projected[:, 0]
            key_new = projected[:, 1]
            val_new = projected[:, 2]
            new_keys.append(key_new)
            new_vals.append(val_new)
            if layer == 0:
                payload = jnp.concatenate([query, group_id.astype(jnp.bfloat16)[:, None]], axis=1)
                gathered = spread(payload, n_req)
                group_all = gathered[:, :, width_here].astype(jnp.int32)
            else:
                gathered = spread(query, n_req)
            query_all = gathered[:, :, :width_here].reshape(n_req, row_count, -1, HD)
            attended = attend(
                query_all,
                query,
                key_new,
                val_new,
                suffix_cache[layer],
                prompt_cache[layer],
                valid,
                page_group,
                group_all,
                n_req,
            )
            partial_value = jnp.dot(attended, w_out[layer], preferred_element_type=jnp.float32)
            residual = residual + head_sum(partial_value, n_head)
            normed = root_norm(residual, gain_mlp[layer]).astype(jnp.bfloat16)
            hidden_units = jax.nn.silu(
                jnp.einsum("rd,fd->rf", normed, w_up[layer], preferred_element_type=jnp.float32)
            ).astype(jnp.bfloat16)
            partial_value = jnp.dot(hidden_units, w_down[layer], preferred_element_type=jnp.float32)
            residual = residual + head_sum(partial_value, n_head)
            if layer + 1 < layer_count:
                normed = root_norm(residual, gain_attn[layer + 1]).astype(jnp.bfloat16)
        hidden = residual.astype(jnp.bfloat16)
        new_cache = jnp.stack([jnp.stack(new_keys), jnp.stack(new_vals)], axis=1)
        return (hidden, new_cache)

    return local


def solution(mesh):
    placed = (
        P("req", None),
        P(None, None, "head", None),
        P(None, "head", None),
        P(None, "head", None),
        P(None, "head", None),
        P(),
        P(),
        P(None, None, "req", "head", None),
        P(None, None, "req", "head", None),
        P("req", None),
        P(),
        P("req"),
        P("req"),
    )
    return jax.shard_map(
        make_local(mesh.shape["req"], mesh.shape["head"]),
        mesh=mesh,
        in_specs=placed,
        out_specs=(P("req", None), P(None, None, "req", "head")),
        check_vma=False,
    )
```

```python
import math

import jax
import jax.numpy as jnp
from jax import lax
from jax.experimental import pallas as pl
from jax.experimental.pallas import tpu as pltpu
from jax.sharding import PartitionSpec as P

HD = 80
PPAGES = 4


NEG_FLOOR = -1e30


def root_norm(values, gains):
    factor = lax.rsqrt(jnp.mean(values * values, axis=-1, keepdims=True) + 1e-06)
    return values * factor * gains


def head_sum(value, count):
    chips = count // 2
    value = value + lax.ppermute(value, "head", [(i, i ^ 1) for i in range(count)])

    def from_chip(shift):
        pairs = [(i, ((i // 2 + shift) % chips) * 2 + i % 2) for i in range(count)]
        return lax.ppermute(value, "head", pairs)

    later = from_chip(1)
    opposite = from_chip(2)
    earlier = from_chip(chips - 1)
    return (value + opposite) + (later + earlier)


def spread(value, count):
    copies = jnp.broadcast_to(value[None], (count,) + value.shape)
    return lax.all_to_all(copies, "req", 0, 0, tiled=True)


def send_home(parts, count):
    return lax.all_to_all(parts, "req", 0, 0, tiled=True)


def softmax_part(scores, mask, values_fn, axes):
    top = jnp.max(jnp.where(mask, scores, NEG_FLOOR), axis=axes)
    expand = top.reshape(top.shape + (1,) * len(axes))
    weights = jnp.exp(jnp.where(mask, scores - expand, NEG_FLOOR))
    total = jnp.sum(weights, axis=axes)
    mixed = values_fn(weights.astype(jnp.bfloat16))
    return top, total, mixed


def pack_part(mixed, top, total, lanes):
    pad = jnp.zeros(mixed.shape[:-1] + (lanes - HD - 2,), jnp.float32)
    return jnp.concatenate([mixed, top[..., None], total[..., None], pad], axis=-1)


def merge_kernel(back_ref, here_ref, w_ref, out_ref):
    head_count = here_ref.shape[0]
    acc = jnp.zeros(out_ref.shape, jnp.float32)
    for h in range(head_count):
        back = back_ref[:, h]
        here = here_ref[h]
        b_top = back[:, :, HD : HD + 1]
        h_top = here[:, HD : HD + 1]
        top = jnp.maximum(jnp.max(b_top, axis=0), h_top)
        b_factor = jnp.exp(b_top - top[None])
        h_factor = jnp.exp(h_top - top)
        total = jnp.sum(back[:, :, HD + 1 : HD + 2] * b_factor, axis=0) + here[:, HD + 1 : HD + 2] * h_factor
        mixed = jnp.sum(back[:, :, :HD] * b_factor, axis=0) + here[:, :HD] * h_factor
        attended = (mixed / total).astype(jnp.bfloat16)
        acc = acc + jnp.dot(attended, w_ref[h * HD : (h + 1) * HD, :], preferred_element_type=jnp.float32)
    out_ref[...] = acc


def merge_project(back, here, w_layer):
    n_src, head_count, rows, lanes = back.shape
    width = w_layer.shape[1]
    return pl.pallas_call(
        merge_kernel,
        out_shape=jax.ShapeDtypeStruct((rows, width), jnp.float32),
        in_specs=[
            pl.BlockSpec(memory_space=pltpu.VMEM),
            pl.BlockSpec(memory_space=pltpu.VMEM),
            pl.BlockSpec(memory_space=pltpu.VMEM),
        ],
        out_specs=pl.BlockSpec(memory_space=pltpu.VMEM),
    )(back, here, w_layer)


def attend_project(query_all, query, key_new, val_new, layer_suffix, layer_prompt, valid, page_group, group_all, n_req, w_layer):
    row_count = query.shape[0]
    head_count = query.shape[1] // HD
    scale = 1.0 / math.sqrt(HD)
    page_len = layer_suffix.shape[3]
    lanes = 128
    query_heads = query.reshape(row_count, head_count, HD)
    key_heads = key_new.reshape(row_count, head_count, HD)
    val_heads = val_new.reshape(row_count, head_count, HD)

    pool = layer_suffix.shape[1]
    s_keys = layer_suffix[0].reshape(pool, head_count, HD, page_len)
    s_vals = layer_suffix[1].reshape(pool, head_count, HD, page_len)
    s_scores = (
        jnp.einsum("ihd,phdt->ihpt", query_heads, s_keys, preferred_element_type=jnp.float32)
        * scale
    )
    s_top, s_total, s_mixed = softmax_part(
        s_scores,
        valid[:, None],
        lambda w: jnp.einsum("ihpt,phdt->ihd", w, s_vals, preferred_element_type=jnp.float32),
        (2, 3),
    )
    own = (
        jnp.einsum("rhd,rhd->rh", query_heads, key_heads, preferred_element_type=jnp.float32)
        * scale
    )
    l_top = jnp.maximum(s_top, own)
    s_factor = jnp.exp(s_top - l_top)
    own_weight = jnp.exp(own - l_top)
    l_total = s_total * s_factor + own_weight
    l_mixed = (
        s_mixed * s_factor[..., None]
        + own_weight.astype(jnp.bfloat16).astype(jnp.float32)[..., None]
        * val_heads.astype(jnp.float32)
    )
    here = pack_part(l_mixed, l_top, l_total, lanes).transpose(1, 0, 2)

    count = layer_prompt.shape[1]
    p_keys = layer_prompt[0].reshape(count, head_count, HD, page_len)
    p_vals = layer_prompt[1].reshape(count, head_count, HD, page_len)
    p_scores = (
        jnp.einsum("sihd,khdt->sihkt", query_all, p_keys, preferred_element_type=jnp.float32)
        * scale
    )
    match = (group_all[:, :, None] == page_group[None, None, :])[:, :, None, :, None]
    p_top, p_total, p_mixed = softmax_part(
        p_scores,
        match,
        lambda w: jnp.einsum("sihkt,khdt->sihd", w, p_vals, preferred_element_type=jnp.float32),
        (3, 4),
    )
    packed = pack_part(p_mixed, p_top, p_total, lanes).transpose(0, 2, 1, 3)
    back = send_home(packed, n_req)
    return merge_project(back, here, w_layer)


def make_local(n_req, n_head):
    def local(
        tokens,
        w_qkv,
        w_out,
        w_up,
        w_down,
        gain_attn,
        gain_mlp,
        suffix_cache,
        prompt_cache,
        suffix_table,
        prompt_owner,
        suffix_len,
        group_id,
    ):
        row_count = tokens.shape[0]
        layer_count = w_qkv.shape[0]
        width_here = w_qkv.shape[2]
        model_width = w_qkv.shape[3]
        page_len = suffix_cache.shape[4]
        pool = suffix_cache.shape[2]
        own_pages = suffix_table.shape[1] // row_count
        prompt_here = prompt_cache.shape[2]

        table = suffix_table[0].reshape(row_count, own_pages)
        rows = jnp.arange(page_len, dtype=jnp.int32)
        page_ids = jnp.arange(pool, dtype=jnp.int32)
        valid = jnp.zeros((row_count, pool, page_len), dtype=bool)
        for slot in range(own_pages):
            chosen = (table[:, slot][:, None] == page_ids[None, :])[:, :, None]
            filled = (slot * page_len + rows)[None, None, :] < suffix_len[:, None, None]
            valid = valid | (chosen & filled)

        here = lax.axis_index("req")
        page_group = lax.dynamic_slice(prompt_owner, (here * prompt_here,), (prompt_here,)) // PPAGES

        whole = tokens.astype(jnp.float32)
        normed = root_norm(whole, gain_attn[0]).astype(jnp.bfloat16)
        residual = whole
        new_keys = []
        new_vals = []
        for layer in range(layer_count):
            projected = jnp.einsum(
                "rd,kd->rk",
                normed,
                w_qkv[layer].reshape(3 * width_here, model_width),
                preferred_element_type=jnp.float32,
            )
            projected = projected.reshape(row_count, 3, width_here).astype(jnp.bfloat16)
            query = projected[:, 0]
            key_new = projected[:, 1]
            val_new = projected[:, 2]
            new_keys.append(key_new)
            new_vals.append(val_new)
            if layer == 0:
                payload = jnp.concatenate([query, group_id.astype(jnp.bfloat16)[:, None]], axis=1)
                gathered = spread(payload, n_req)
                group_all = gathered[:, :, width_here].astype(jnp.int32)
            else:
                gathered = spread(query, n_req)
            query_all = gathered[:, :, :width_here].reshape(n_req, row_count, -1, HD)
            partial_value = attend_project(
                query_all,
                query,
                key_new,
                val_new,
                suffix_cache[layer],
                prompt_cache[layer],
                valid,
                page_group,
                group_all,
                n_req,
                w_out[layer],
            )
            residual = residual + head_sum(partial_value, n_head)
            normed = root_norm(residual, gain_mlp[layer]).astype(jnp.bfloat16)
            hidden_units = jax.nn.silu(
                jnp.einsum("rd,fd->rf", normed, w_up[layer], preferred_element_type=jnp.float32)
            ).astype(jnp.bfloat16)
            partial_value = jnp.dot(hidden_units, w_down[layer], preferred_element_type=jnp.float32)
            residual = residual + head_sum(partial_value, n_head)
            if layer + 1 < layer_count:
                normed = root_norm(residual, gain_attn[layer + 1]).astype(jnp.bfloat16)
        hidden = residual.astype(jnp.bfloat16)
        new_cache = jnp.stack([jnp.stack(new_keys), jnp.stack(new_vals)], axis=1)
        return (hidden, new_cache)

    return local


def solution(mesh):
    placed = (
        P("req", None),
        P(None, None, "head", None),
        P(None, "head", None),
        P(None, "head", None),
        P(None, "head", None),
        P(),
        P(),
        P(None, None, "req", "head", None),
        P(None, None, "req", "head", None),
        P("req", None),
        P(),
        P("req"),
        P("req"),
    )
    return jax.shard_map(
        make_local(mesh.shape["req"], mesh.shape["head"]),
        mesh=mesh,
        in_specs=placed,
        out_specs=(P("req", None), P(None, None, "req", "head")),
        check_vma=False,
    )
```

```python
import math

import jax
import jax.numpy as jnp
from jax import lax
from jax.experimental import pallas as pl
from jax.experimental.pallas import tpu as pltpu
from jax.sharding import PartitionSpec as P

HD = 80
PPAGES = 4


NEG_FLOOR = -1e30


def root_norm(values, gains):
    factor = lax.rsqrt(jnp.mean(values * values, axis=-1, keepdims=True) + 1e-06)
    return values * factor * gains


def head_sum(value, count):
    chips = count // 2
    value = value + lax.ppermute(value, "head", [(i, i ^ 1) for i in range(count)])

    def from_chip(shift):
        pairs = [(i, ((i // 2 + shift) % chips) * 2 + i % 2) for i in range(count)]
        return lax.ppermute(value, "head", pairs)

    later = from_chip(1)
    opposite = from_chip(2)
    earlier = from_chip(chips - 1)
    return (value + opposite) + (later + earlier)


def spread(value, count):
    copies = jnp.broadcast_to(value[None], (count,) + value.shape)
    return lax.all_to_all(copies, "req", 0, 0, tiled=True)


def send_home(parts, count):
    return lax.all_to_all(parts, "req", 0, 0, tiled=True)


def softmax_part(scores, mask, values_fn, axes):
    top = jnp.max(jnp.where(mask, scores, NEG_FLOOR), axis=axes)
    expand = top.reshape(top.shape + (1,) * len(axes))
    weights = jnp.exp(jnp.where(mask, scores - expand, NEG_FLOOR))
    total = jnp.sum(weights, axis=axes)
    mixed = values_fn(weights.astype(jnp.bfloat16))
    return top, total, mixed


def pack_part(mixed, top, total, lanes):
    pad = jnp.zeros(mixed.shape[:-1] + (lanes - HD - 2,), jnp.float32)
    return jnp.concatenate([mixed, top[..., None], total[..., None], pad], axis=-1)


def merge_kernel(back_ref, here_ref, w_ref, out_ref):
    head_count = here_ref.shape[0]
    acc = jnp.zeros(out_ref.shape, jnp.float32)
    for h in range(head_count):
        back = back_ref[:, h]
        here = here_ref[h]
        b_top = back[:, :, HD : HD + 1]
        h_top = here[:, HD : HD + 1]
        top = jnp.maximum(jnp.max(b_top, axis=0), h_top)
        b_factor = jnp.exp(b_top - top[None])
        h_factor = jnp.exp(h_top - top)
        total = jnp.sum(back[:, :, HD + 1 : HD + 2] * b_factor, axis=0) + here[:, HD + 1 : HD + 2] * h_factor
        mixed = jnp.sum(back[:, :, :HD] * b_factor, axis=0) + here[:, :HD] * h_factor
        attended = (mixed / total).astype(jnp.bfloat16)
        acc = acc + jnp.dot(attended, w_ref[h * HD : (h + 1) * HD, :], preferred_element_type=jnp.float32)
    out_ref[...] = acc


def merge_project(back, here, w_layer):
    n_src, head_count, rows, lanes = back.shape
    width = w_layer.shape[1]
    return pl.pallas_call(
        merge_kernel,
        out_shape=jax.ShapeDtypeStruct((rows, width), jnp.float32),
        in_specs=[
            pl.BlockSpec(memory_space=pltpu.VMEM),
            pl.BlockSpec(memory_space=pltpu.VMEM),
            pl.BlockSpec(memory_space=pltpu.VMEM),
        ],
        out_specs=pl.BlockSpec(memory_space=pltpu.VMEM),
    )(back, here, w_layer)


def local_part(query_heads, key_new, val_new, layer_suffix, valid, lanes):
    row_count, head_count, _ = query_heads.shape
    scale = 1.0 / math.sqrt(HD)
    page_len = layer_suffix.shape[3]
    key_heads = key_new.reshape(row_count, head_count, HD)
    val_heads = val_new.reshape(row_count, head_count, HD)
    pool = layer_suffix.shape[1]
    s_keys = layer_suffix[0].reshape(pool, head_count, HD, page_len)
    s_vals = layer_suffix[1].reshape(pool, head_count, HD, page_len)
    s_scores = (
        jnp.einsum("ihd,phdt->ihpt", query_heads, s_keys, preferred_element_type=jnp.float32)
        * scale
    )
    s_top, s_total, s_mixed = softmax_part(
        s_scores,
        valid[:, None],
        lambda w: jnp.einsum("ihpt,phdt->ihd", w, s_vals, preferred_element_type=jnp.float32),
        (2, 3),
    )
    own = (
        jnp.einsum("rhd,rhd->rh", query_heads, key_heads, preferred_element_type=jnp.float32)
        * scale
    )
    l_top = jnp.maximum(s_top, own)
    s_factor = jnp.exp(s_top - l_top)
    own_weight = jnp.exp(own - l_top)
    l_total = s_total * s_factor + own_weight
    l_mixed = (
        s_mixed * s_factor[..., None]
        + own_weight.astype(jnp.bfloat16).astype(jnp.float32)[..., None]
        * val_heads.astype(jnp.float32)
    )
    return pack_part(l_mixed, l_top, l_total, lanes).transpose(1, 0, 2)


def attend_project(query_all, query, key_new, val_new, layer_suffix, layer_prompt, valid, page_group, group_all, n_req, w_layer):
    row_count = query.shape[0]
    head_count = query.shape[1] // HD
    scale = 1.0 / math.sqrt(HD)
    page_len = layer_suffix.shape[3]
    lanes = 128
    query_heads = query.reshape(row_count, head_count, HD)
    key_heads = key_new.reshape(row_count, head_count, HD)
    val_heads = val_new.reshape(row_count, head_count, HD)

    here = local_part(query_heads, key_new, val_new, layer_suffix, valid, lanes)

    count = layer_prompt.shape[1]
    p_keys = layer_prompt[0].reshape(count, head_count, HD, page_len)
    p_vals = layer_prompt[1].reshape(count, head_count, HD, page_len)
    p_scores = (
        jnp.einsum("sihd,khdt->sihkt", query_all, p_keys, preferred_element_type=jnp.float32)
        * scale
    )
    match = (group_all[:, :, None] == page_group[None, None, :])[:, :, None, :, None]
    p_top, p_total, p_mixed = softmax_part(
        p_scores,
        match,
        lambda w: jnp.einsum("sihkt,khdt->sihd", w, p_vals, preferred_element_type=jnp.float32),
        (3, 4),
    )
    packed = pack_part(p_mixed, p_top, p_total, lanes).transpose(0, 2, 1, 3)
    back = send_home(packed, n_req)
    return merge_project(back, here, w_layer)


def attend_gathered(query, key_new, val_new, layer_suffix, gathered_prompt, valid, group_id, prompt_owner, w_layer):
    row_count = query.shape[0]
    head_count = query.shape[1] // HD
    scale = 1.0 / math.sqrt(HD)
    page_len = layer_suffix.shape[3]
    lanes = 128
    query_heads = query.reshape(row_count, head_count, HD)
    here = local_part(query_heads, key_new, val_new, layer_suffix, valid, lanes)
    count = gathered_prompt.shape[1]
    p_keys = gathered_prompt[0].reshape(count, head_count, HD, page_len)
    p_vals = gathered_prompt[1].reshape(count, head_count, HD, page_len)
    p_scores = (
        jnp.einsum("ihd,khdt->ihkt", query_heads, p_keys, preferred_element_type=jnp.float32)
        * scale
    )
    match = (group_id[:, None] == (prompt_owner // PPAGES)[None, :])[:, None, :, None]
    p_top, p_total, p_mixed = softmax_part(
        p_scores,
        match,
        lambda w: jnp.einsum("ihkt,khdt->ihd", w, p_vals, preferred_element_type=jnp.float32),
        (2, 3),
    )
    back = pack_part(p_mixed, p_top, p_total, lanes).transpose(1, 0, 2)[None]
    return merge_project(back, here, w_layer)


def make_local(n_req, n_head):
    def local(
        tokens,
        w_qkv,
        w_out,
        w_up,
        w_down,
        gain_attn,
        gain_mlp,
        suffix_cache,
        prompt_cache,
        suffix_table,
        prompt_owner,
        suffix_len,
        group_id,
    ):
        row_count = tokens.shape[0]
        layer_count = w_qkv.shape[0]
        width_here = w_qkv.shape[2]
        model_width = w_qkv.shape[3]
        page_len = suffix_cache.shape[4]
        pool = suffix_cache.shape[2]
        own_pages = suffix_table.shape[1] // row_count
        prompt_here = prompt_cache.shape[2]

        table = suffix_table[0].reshape(row_count, own_pages)
        rows = jnp.arange(page_len, dtype=jnp.int32)
        page_ids = jnp.arange(pool, dtype=jnp.int32)
        valid = jnp.zeros((row_count, pool, page_len), dtype=bool)
        for slot in range(own_pages):
            chosen = (table[:, slot][:, None] == page_ids[None, :])[:, :, None]
            filled = (slot * page_len + rows)[None, None, :] < suffix_len[:, None, None]
            valid = valid | (chosen & filled)

        here = lax.axis_index("req")
        page_group = lax.dynamic_slice(prompt_owner, (here * prompt_here,), (prompt_here,)) // PPAGES

        last_prompt = lax.all_gather(prompt_cache[layer_count - 1], "req", axis=1, tiled=True)
        whole = tokens.astype(jnp.float32)
        normed = root_norm(whole, gain_attn[0]).astype(jnp.bfloat16)
        residual = whole
        new_keys = []
        new_vals = []
        for layer in range(layer_count):
            projected = jnp.einsum(
                "rd,kd->rk",
                normed,
                w_qkv[layer].reshape(3 * width_here, model_width),
                preferred_element_type=jnp.float32,
            )
            projected = projected.reshape(row_count, 3, width_here).astype(jnp.bfloat16)
            query = projected[:, 0]
            key_new = projected[:, 1]
            val_new = projected[:, 2]
            new_keys.append(key_new)
            new_vals.append(val_new)
            if layer == layer_count - 1 and layer > 0:
                partial_value = attend_gathered(
                    query, key_new, val_new, suffix_cache[layer], last_prompt, valid,
                    group_id, prompt_owner, w_out[layer],
                )
            elif layer == 0:
                payload = jnp.concatenate([query, group_id.astype(jnp.bfloat16)[:, None]], axis=1)
                gathered = spread(payload, n_req)
                group_all = gathered[:, :, width_here].astype(jnp.int32)
            else:
                gathered = spread(query, n_req)
            if layer < layer_count - 1 or layer == 0:
              query_all = gathered[:, :, :width_here].reshape(n_req, row_count, -1, HD)
              partial_value = attend_project(
                query_all,
                query,
                key_new,
                val_new,
                suffix_cache[layer],
                prompt_cache[layer],
                valid,
                page_group,
                group_all,
                n_req,
                w_out[layer],
            )
            residual = residual + head_sum(partial_value, n_head)
            normed = root_norm(residual, gain_mlp[layer]).astype(jnp.bfloat16)
            hidden_units = jax.nn.silu(
                jnp.einsum("rd,fd->rf", normed, w_up[layer], preferred_element_type=jnp.float32)
            ).astype(jnp.bfloat16)
            partial_value = jnp.dot(hidden_units, w_down[layer], preferred_element_type=jnp.float32)
            residual = residual + head_sum(partial_value, n_head)
            if layer + 1 < layer_count:
                normed = root_norm(residual, gain_attn[layer + 1]).astype(jnp.bfloat16)
        hidden = residual.astype(jnp.bfloat16)
        new_cache = jnp.stack([jnp.stack(new_keys), jnp.stack(new_vals)], axis=1)
        return (hidden, new_cache)

    return local


def solution(mesh):
    placed = (
        P("req", None),
        P(None, None, "head", None),
        P(None, "head", None),
        P(None, "head", None),
        P(None, "head", None),
        P(),
        P(),
        P(None, None, "req", "head", None),
        P(None, None, "req", "head", None),
        P("req", None),
        P(),
        P("req"),
        P("req"),
    )
    return jax.shard_map(
        make_local(mesh.shape["req"], mesh.shape["head"]),
        mesh=mesh,
        in_specs=placed,
        out_specs=(P("req", None), P(None, None, "req", "head")),
        check_vma=False,
    )
```

```python
import math

import jax
import jax.numpy as jnp
from jax import lax
from jax.experimental import pallas as pl
from jax.experimental.pallas import tpu as pltpu
from jax.sharding import PartitionSpec as P

HD = 80
PPAGES = 4


NEG_FLOOR = -1e30


def root_norm(values, gains):
    factor = lax.rsqrt(jnp.mean(values * values, axis=-1, keepdims=True) + 1e-06)
    return values * factor * gains


def head_sum(value, count):
    chips = count // 2
    value = value + lax.ppermute(value, "head", [(i, i ^ 1) for i in range(count)])

    def from_chip(shift):
        pairs = [(i, ((i // 2 + shift) % chips) * 2 + i % 2) for i in range(count)]
        return lax.ppermute(value, "head", pairs)

    later = from_chip(1)
    opposite = from_chip(2)
    earlier = from_chip(chips - 1)
    return (value + opposite) + (later + earlier)


def spread(value, count):
    copies = jnp.broadcast_to(value[None], (count,) + value.shape)
    return lax.all_to_all(copies, "req", 0, 0, tiled=True)


def send_home(parts, count):
    return lax.all_to_all(parts, "req", 0, 0, tiled=True)


def softmax_part(scores, mask, values_fn, axes):
    top = jnp.max(jnp.where(mask, scores, NEG_FLOOR), axis=axes)
    expand = top.reshape(top.shape + (1,) * len(axes))
    weights = jnp.exp(jnp.where(mask, scores - expand, NEG_FLOOR))
    total = jnp.sum(weights, axis=axes)
    mixed = values_fn(weights.astype(jnp.bfloat16))
    return top, total, mixed


def pack_part(mixed, top, total, lanes):
    pad = jnp.zeros(mixed.shape[:-1] + (lanes - HD - 2,), jnp.float32)
    return jnp.concatenate([mixed, top[..., None], total[..., None], pad], axis=-1)


def merge_kernel(back_ref, here_ref, w_ref, out_ref):
    head_count = here_ref.shape[0]
    acc = jnp.zeros(out_ref.shape, jnp.float32)
    for h in range(head_count):
        back = back_ref[:, h]
        here = here_ref[h]
        b_top = back[:, :, HD : HD + 1]
        h_top = here[:, HD : HD + 1]
        top = jnp.maximum(jnp.max(b_top, axis=0), h_top)
        b_factor = jnp.exp(b_top - top[None])
        h_factor = jnp.exp(h_top - top)
        total = jnp.sum(back[:, :, HD + 1 : HD + 2] * b_factor, axis=0) + here[:, HD + 1 : HD + 2] * h_factor
        mixed = jnp.sum(back[:, :, :HD] * b_factor, axis=0) + here[:, :HD] * h_factor
        attended = (mixed / total).astype(jnp.bfloat16)
        acc = acc + jnp.dot(attended, w_ref[h * HD : (h + 1) * HD, :], preferred_element_type=jnp.float32)
    out_ref[...] = acc


def merge_project(back, here, w_layer):
    n_src, head_count, rows, lanes = back.shape
    width = w_layer.shape[1]
    return pl.pallas_call(
        merge_kernel,
        out_shape=jax.ShapeDtypeStruct((rows, width), jnp.float32),
        in_specs=[
            pl.BlockSpec(memory_space=pltpu.VMEM),
            pl.BlockSpec(memory_space=pltpu.VMEM),
            pl.BlockSpec(memory_space=pltpu.VMEM),
        ],
        out_specs=pl.BlockSpec(memory_space=pltpu.VMEM),
    )(back, here, w_layer)


def local_part(query_heads, key_new, val_new, layer_suffix, valid, lanes):
    row_count, head_count, _ = query_heads.shape
    scale = 1.0 / math.sqrt(HD)
    page_len = layer_suffix.shape[3]
    key_heads = key_new.reshape(row_count, head_count, HD)
    val_heads = val_new.reshape(row_count, head_count, HD)
    pool = layer_suffix.shape[1]
    s_keys = layer_suffix[0].reshape(pool, head_count, HD, page_len)
    s_vals = layer_suffix[1].reshape(pool, head_count, HD, page_len)
    s_scores = (
        jnp.einsum("ihd,phdt->ihpt", query_heads, s_keys, preferred_element_type=jnp.float32)
        * scale
    )
    s_top, s_total, s_mixed = softmax_part(
        s_scores,
        valid[:, None],
        lambda w: jnp.einsum("ihpt,phdt->ihd", w, s_vals, preferred_element_type=jnp.float32),
        (2, 3),
    )
    own = (
        jnp.einsum("rhd,rhd->rh", query_heads, key_heads, preferred_element_type=jnp.float32)
        * scale
    )
    l_top = jnp.maximum(s_top, own)
    s_factor = jnp.exp(s_top - l_top)
    own_weight = jnp.exp(own - l_top)
    l_total = s_total * s_factor + own_weight
    l_mixed = (
        s_mixed * s_factor[..., None]
        + own_weight.astype(jnp.bfloat16).astype(jnp.float32)[..., None]
        * val_heads.astype(jnp.float32)
    )
    return pack_part(l_mixed, l_top, l_total, lanes).transpose(1, 0, 2)


def attend_project(query_all, query, key_new, val_new, layer_suffix, layer_prompt, valid, page_group, group_all, n_req, w_layer):
    row_count = query.shape[0]
    head_count = query.shape[1] // HD
    scale = 1.0 / math.sqrt(HD)
    page_len = layer_suffix.shape[3]
    lanes = 128
    query_heads = query.reshape(row_count, head_count, HD)
    key_heads = key_new.reshape(row_count, head_count, HD)
    val_heads = val_new.reshape(row_count, head_count, HD)

    here = local_part(query_heads, key_new, val_new, layer_suffix, valid, lanes)

    count = layer_prompt.shape[1]
    p_keys = layer_prompt[0].reshape(count, head_count, HD, page_len)
    p_vals = layer_prompt[1].reshape(count, head_count, HD, page_len)
    p_scores = (
        jnp.einsum("sihd,khdt->sihkt", query_all, p_keys, preferred_element_type=jnp.float32)
        * scale
    )
    match = (group_all[:, :, None] == page_group[None, None, :])[:, :, None, :, None]
    p_top, p_total, p_mixed = softmax_part(
        p_scores,
        match,
        lambda w: jnp.einsum("sihkt,khdt->sihd", w, p_vals, preferred_element_type=jnp.float32),
        (3, 4),
    )
    packed = pack_part(p_mixed, p_top, p_total, lanes).transpose(0, 2, 1, 3)
    back = send_home(packed, n_req)
    return merge_project(back, here, w_layer)


def attend_gathered(query, key_new, val_new, layer_suffix, gathered_prompt, valid, group_id, prompt_owner, w_layer):
    row_count = query.shape[0]
    head_count = query.shape[1] // HD
    scale = 1.0 / math.sqrt(HD)
    page_len = layer_suffix.shape[3]
    lanes = 128
    query_heads = query.reshape(row_count, head_count, HD)
    here = local_part(query_heads, key_new, val_new, layer_suffix, valid, lanes)
    count = gathered_prompt.shape[0] * gathered_prompt.shape[2]
    p_keys = gathered_prompt[:, 0].reshape(count, head_count, HD, page_len)
    p_vals = gathered_prompt[:, 1].reshape(count, head_count, HD, page_len)
    p_scores = (
        jnp.einsum("ihd,khdt->ihkt", query_heads, p_keys, preferred_element_type=jnp.float32)
        * scale
    )
    match = (group_id[:, None] == (prompt_owner // PPAGES)[None, :])[:, None, :, None]
    p_top, p_total, p_mixed = softmax_part(
        p_scores,
        match,
        lambda w: jnp.einsum("ihkt,khdt->ihd", w, p_vals, preferred_element_type=jnp.float32),
        (2, 3),
    )
    back = pack_part(p_mixed, p_top, p_total, lanes).transpose(1, 0, 2)[None]
    return merge_project(back, here, w_layer)


def make_local(n_req, n_head):
    def local(
        tokens,
        w_qkv,
        w_out,
        w_up,
        w_down,
        gain_attn,
        gain_mlp,
        suffix_cache,
        prompt_cache,
        suffix_table,
        prompt_owner,
        suffix_len,
        group_id,
    ):
        row_count = tokens.shape[0]
        layer_count = w_qkv.shape[0]
        width_here = w_qkv.shape[2]
        model_width = w_qkv.shape[3]
        page_len = suffix_cache.shape[4]
        pool = suffix_cache.shape[2]
        own_pages = suffix_table.shape[1] // row_count
        prompt_here = prompt_cache.shape[2]

        table = suffix_table[0].reshape(row_count, own_pages)
        rows = jnp.arange(page_len, dtype=jnp.int32)
        page_ids = jnp.arange(pool, dtype=jnp.int32)
        valid = jnp.zeros((row_count, pool, page_len), dtype=bool)
        for slot in range(own_pages):
            chosen = (table[:, slot][:, None] == page_ids[None, :])[:, :, None]
            filled = (slot * page_len + rows)[None, None, :] < suffix_len[:, None, None]
            valid = valid | (chosen & filled)

        here = lax.axis_index("req")
        page_group = lax.dynamic_slice(prompt_owner, (here * prompt_here,), (prompt_here,)) // PPAGES

        last_prompt = spread(prompt_cache[layer_count - 1], n_req)
        whole = tokens.astype(jnp.float32)
        normed = root_norm(whole, gain_attn[0]).astype(jnp.bfloat16)
        residual = whole
        new_keys = []
        new_vals = []
        for layer in range(layer_count):
            projected = jnp.einsum(
                "rd,kd->rk",
                normed,
                w_qkv[layer].reshape(3 * width_here, model_width),
                preferred_element_type=jnp.float32,
            )
            projected = projected.reshape(row_count, 3, width_here).astype(jnp.bfloat16)
            query = projected[:, 0]
            key_new = projected[:, 1]
            val_new = projected[:, 2]
            new_keys.append(key_new)
            new_vals.append(val_new)
            if layer == layer_count - 1 and layer > 0:
                partial_value = attend_gathered(
                    query, key_new, val_new, suffix_cache[layer], last_prompt, valid,
                    group_id, prompt_owner, w_out[layer],
                )
            elif layer == 0:
                payload = jnp.concatenate([query, group_id.astype(jnp.bfloat16)[:, None]], axis=1)
                gathered = spread(payload, n_req)
                group_all = gathered[:, :, width_here].astype(jnp.int32)
            else:
                gathered = spread(query, n_req)
            if layer < layer_count - 1 or layer == 0:
              query_all = gathered[:, :, :width_here].reshape(n_req, row_count, -1, HD)
              partial_value = attend_project(
                query_all,
                query,
                key_new,
                val_new,
                suffix_cache[layer],
                prompt_cache[layer],
                valid,
                page_group,
                group_all,
                n_req,
                w_out[layer],
            )
            residual = residual + head_sum(partial_value, n_head)
            normed = root_norm(residual, gain_mlp[layer]).astype(jnp.bfloat16)
            hidden_units = jax.nn.silu(
                jnp.einsum("rd,fd->rf", normed, w_up[layer], preferred_element_type=jnp.float32)
            ).astype(jnp.bfloat16)
            partial_value = jnp.dot(hidden_units, w_down[layer], preferred_element_type=jnp.float32)
            residual = residual + head_sum(partial_value, n_head)
            if layer + 1 < layer_count:
                normed = root_norm(residual, gain_attn[layer + 1]).astype(jnp.bfloat16)
        hidden = residual.astype(jnp.bfloat16)
        new_cache = jnp.stack([jnp.stack(new_keys), jnp.stack(new_vals)], axis=1)
        return (hidden, new_cache)

    return local


def solution(mesh):
    placed = (
        P("req", None),
        P(None, None, "head", None),
        P(None, "head", None),
        P(None, "head", None),
        P(None, "head", None),
        P(),
        P(),
        P(None, None, "req", "head", None),
        P(None, None, "req", "head", None),
        P("req", None),
        P(),
        P("req"),
        P("req"),
    )
    return jax.shard_map(
        make_local(mesh.shape["req"], mesh.shape["head"]),
        mesh=mesh,
        in_specs=placed,
        out_specs=(P("req", None), P(None, None, "req", "head")),
        check_vma=False,
    )
```

```python
import math

import jax
import jax.numpy as jnp
from jax import lax
from jax.experimental import pallas as pl
from jax.experimental.pallas import tpu as pltpu
from jax.sharding import PartitionSpec as P

HD = 80
PPAGES = 4


NEG_FLOOR = -1e30


def root_norm(values, gains):
    factor = lax.rsqrt(jnp.mean(values * values, axis=-1, keepdims=True) + 1e-06)
    return values * factor * gains


def head_sum(value, count):
    chips = count // 2
    value = value + lax.ppermute(value, "head", [(i, i ^ 1) for i in range(count)])

    def from_chip(shift):
        pairs = [(i, ((i // 2 + shift) % chips) * 2 + i % 2) for i in range(count)]
        return lax.ppermute(value, "head", pairs)

    later = from_chip(1)
    opposite = from_chip(2)
    earlier = from_chip(chips - 1)
    return (value + opposite) + (later + earlier)


def spread(value, count):
    copies = jnp.broadcast_to(value[None], (count,) + value.shape)
    return lax.all_to_all(copies, "req", 0, 0, tiled=True)


def send_home(parts, count):
    return lax.all_to_all(parts, "req", 0, 0, tiled=True)


def softmax_part(scores, mask, values_fn, axes):
    top = jnp.max(jnp.where(mask, scores, NEG_FLOOR), axis=axes)
    expand = top.reshape(top.shape + (1,) * len(axes))
    weights = jnp.exp(jnp.where(mask, scores - expand, NEG_FLOOR))
    total = jnp.sum(weights, axis=axes)
    mixed = values_fn(weights.astype(jnp.bfloat16))
    return top, total, mixed


def pack_part(mixed, top, total, lanes):
    pad = jnp.zeros(mixed.shape[:-1] + (lanes - HD - 2,), jnp.float32)
    return jnp.concatenate([mixed, top[..., None], total[..., None], pad], axis=-1)


def merge_kernel(back_ref, here_ref, w_ref, out_ref):
    head_count = here_ref.shape[0]
    acc = jnp.zeros(out_ref.shape, jnp.float32)
    for h in range(head_count):
        back = back_ref[:, h]
        here = here_ref[h]
        b_top = back[:, :, HD : HD + 1]
        h_top = here[:, HD : HD + 1]
        top = jnp.maximum(jnp.max(b_top, axis=0), h_top)
        b_factor = jnp.exp(b_top - top[None])
        h_factor = jnp.exp(h_top - top)
        total = jnp.sum(back[:, :, HD + 1 : HD + 2] * b_factor, axis=0) + here[:, HD + 1 : HD + 2] * h_factor
        mixed = jnp.sum(back[:, :, :HD] * b_factor, axis=0) + here[:, :HD] * h_factor
        attended = (mixed / total).astype(jnp.bfloat16)
        acc = acc + jnp.dot(attended, w_ref[h * HD : (h + 1) * HD, :], preferred_element_type=jnp.float32)
    out_ref[...] = acc


def merge_project(back, here, w_layer):
    n_src, head_count, rows, lanes = back.shape
    width = w_layer.shape[1]
    return pl.pallas_call(
        merge_kernel,
        out_shape=jax.ShapeDtypeStruct((rows, width), jnp.float32),
        in_specs=[
            pl.BlockSpec(memory_space=pltpu.VMEM),
            pl.BlockSpec(memory_space=pltpu.VMEM),
            pl.BlockSpec(memory_space=pltpu.VMEM),
        ],
        out_specs=pl.BlockSpec(memory_space=pltpu.VMEM),
    )(back, here, w_layer)


def local_part(query_heads, key_new, val_new, layer_suffix, valid, lanes):
    row_count, head_count, _ = query_heads.shape
    scale = 1.0 / math.sqrt(HD)
    page_len = layer_suffix.shape[3]
    key_heads = key_new.reshape(row_count, head_count, HD)
    val_heads = val_new.reshape(row_count, head_count, HD)
    pool = layer_suffix.shape[1]
    s_keys = layer_suffix[0].reshape(pool, head_count, HD, page_len)
    s_vals = layer_suffix[1].reshape(pool, head_count, HD, page_len)
    s_scores = (
        jnp.einsum("ihd,phdt->ihpt", query_heads, s_keys, preferred_element_type=jnp.float32)
        * scale
    )
    s_top, s_total, s_mixed = softmax_part(
        s_scores,
        valid[:, None],
        lambda w: jnp.einsum("ihpt,phdt->ihd", w, s_vals, preferred_element_type=jnp.float32),
        (2, 3),
    )
    own = (
        jnp.einsum("rhd,rhd->rh", query_heads, key_heads, preferred_element_type=jnp.float32)
        * scale
    )
    l_top = jnp.maximum(s_top, own)
    s_factor = jnp.exp(s_top - l_top)
    own_weight = jnp.exp(own - l_top)
    l_total = s_total * s_factor + own_weight
    l_mixed = (
        s_mixed * s_factor[..., None]
        + own_weight.astype(jnp.bfloat16).astype(jnp.float32)[..., None]
        * val_heads.astype(jnp.float32)
    )
    return pack_part(l_mixed, l_top, l_total, lanes).transpose(1, 0, 2)


def page_kernel(q_ref, pg_ref, kv_ref, out_ref):
    n_src, rows, cols = q_ref.shape
    width = kv_ref.shape[2]
    head_count = width // HD
    pages = kv_ref.shape[1]
    scale = 1.0 / math.sqrt(HD)
    q = q_ref[:, :, 0:width].astype(jnp.float32).reshape(n_src * rows, width)
    group = q_ref[:, :, width : width + 1].astype(jnp.float32).reshape(n_src * rows, 1)
    lane = lax.broadcasted_iota(jnp.int32, q.shape, 1)
    out_ref[...] = jnp.zeros(out_ref.shape, jnp.float32)
    for h in range(head_count):
        inside = (lane >= h * HD) & (lane < (h + 1) * HD)
        q_head = jnp.where(inside, q, 0.0).astype(jnp.bfloat16)
        scores = []
        masks = []
        top = jnp.full((n_src * rows, 1), NEG_FLOOR, jnp.float32)
        for k in range(pages):
            score = jnp.dot(q_head, kv_ref[0, k], preferred_element_type=jnp.float32) * scale
            mask = group == pg_ref[0:1, k : k + 1]
            top = jnp.maximum(top, jnp.max(jnp.where(mask, score, NEG_FLOOR), axis=1, keepdims=True))
            scores.append(score)
            masks.append(mask)
        total = jnp.zeros((n_src * rows, 1), jnp.float32)
        mixed = jnp.zeros((n_src * rows, HD), jnp.float32)
        for k in range(pages):
            weight = jnp.exp(jnp.where(masks[k], scores[k] - top, NEG_FLOOR))
            total = total + jnp.sum(weight, axis=1, keepdims=True)
            mixed = mixed + lax.dot_general(
                weight.astype(jnp.bfloat16),
                kv_ref[1, k, h * HD : (h + 1) * HD, :],
                (((1,), (1,)), ((), ())),
                preferred_element_type=jnp.float32,
            )
        out_ref[:, h, :, 0:HD] = mixed.reshape(n_src, rows, HD)
        out_ref[:, h, :, HD : HD + 1] = top.reshape(n_src, rows, 1)
        out_ref[:, h, :, HD + 1 : HD + 2] = total.reshape(n_src, rows, 1)


def page_partials(payload, page_group, layer_prompt, lanes):
    n_src, rows, _ = payload.shape
    width = layer_prompt.shape[2]
    groups = jnp.zeros((8, lanes), jnp.float32).at[0, : page_group.shape[0]].set(page_group.astype(jnp.float32))
    return pl.pallas_call(
        page_kernel,
        out_shape=jax.ShapeDtypeStruct((n_src, width // HD, rows, lanes), jnp.float32),
        in_specs=[pl.BlockSpec(memory_space=pltpu.VMEM)] * 3,
        out_specs=pl.BlockSpec(memory_space=pltpu.VMEM),
    )(payload, groups, layer_prompt)


def attend_project(payload, query, key_new, val_new, layer_suffix, layer_prompt, valid, page_group, n_req, w_layer):
    row_count = query.shape[0]
    head_count = query.shape[1] // HD
    scale = 1.0 / math.sqrt(HD)
    page_len = layer_suffix.shape[3]
    lanes = 128
    query_heads = query.reshape(row_count, head_count, HD)
    key_heads = key_new.reshape(row_count, head_count, HD)
    val_heads = val_new.reshape(row_count, head_count, HD)

    here = local_part(query_heads, key_new, val_new, layer_suffix, valid, lanes)

    packed = page_partials(payload, page_group, layer_prompt, lanes)
    back = send_home(packed, n_req)
    return merge_project(back, here, w_layer)


def attend_gathered(query, key_new, val_new, layer_suffix, gathered_prompt, valid, group_id, prompt_owner, w_layer):
    row_count = query.shape[0]
    head_count = query.shape[1] // HD
    scale = 1.0 / math.sqrt(HD)
    page_len = layer_suffix.shape[3]
    lanes = 128
    query_heads = query.reshape(row_count, head_count, HD)
    here = local_part(query_heads, key_new, val_new, layer_suffix, valid, lanes)
    count = gathered_prompt.shape[1]
    p_keys = gathered_prompt[0].reshape(count, head_count, HD, page_len)
    p_vals = gathered_prompt[1].reshape(count, head_count, HD, page_len)
    p_scores = (
        jnp.einsum("ihd,khdt->ihkt", query_heads, p_keys, preferred_element_type=jnp.float32)
        * scale
    )
    match = (group_id[:, None] == (prompt_owner // PPAGES)[None, :])[:, None, :, None]
    p_top, p_total, p_mixed = softmax_part(
        p_scores,
        match,
        lambda w: jnp.einsum("ihkt,khdt->ihd", w, p_vals, preferred_element_type=jnp.float32),
        (2, 3),
    )
    back = pack_part(p_mixed, p_top, p_total, lanes).transpose(1, 0, 2)[None]
    return merge_project(back, here, w_layer)


def payload_of(query, group_id):
    return jnp.concatenate([query, group_id.astype(jnp.bfloat16)[:, None]], axis=1)


def make_local(n_req, n_head):
    def local(
        tokens,
        w_qkv,
        w_out,
        w_up,
        w_down,
        gain_attn,
        gain_mlp,
        suffix_cache,
        prompt_cache,
        suffix_table,
        prompt_owner,
        suffix_len,
        group_id,
    ):
        row_count = tokens.shape[0]
        layer_count = w_qkv.shape[0]
        width_here = w_qkv.shape[2]
        model_width = w_qkv.shape[3]
        page_len = suffix_cache.shape[4]
        pool = suffix_cache.shape[2]
        own_pages = suffix_table.shape[1] // row_count
        prompt_here = prompt_cache.shape[2]

        table = suffix_table[0].reshape(row_count, own_pages)
        rows = jnp.arange(page_len, dtype=jnp.int32)
        page_ids = jnp.arange(pool, dtype=jnp.int32)
        valid = jnp.zeros((row_count, pool, page_len), dtype=bool)
        for slot in range(own_pages):
            chosen = (table[:, slot][:, None] == page_ids[None, :])[:, :, None]
            filled = (slot * page_len + rows)[None, None, :] < suffix_len[:, None, None]
            valid = valid | (chosen & filled)

        here = lax.axis_index("req")
        page_group = lax.dynamic_slice(prompt_owner, (here * prompt_here,), (prompt_here,)) // PPAGES

        last_prompt = lax.all_gather(prompt_cache[layer_count - 1], "req", axis=1, tiled=True)
        whole = tokens.astype(jnp.float32)
        normed = root_norm(whole, gain_attn[0]).astype(jnp.bfloat16)
        residual = whole
        new_keys = []
        new_vals = []
        for layer in range(layer_count):
            projected = jnp.einsum(
                "rd,kd->rk",
                normed,
                w_qkv[layer].reshape(3 * width_here, model_width),
                preferred_element_type=jnp.float32,
            )
            projected = projected.reshape(row_count, 3, width_here).astype(jnp.bfloat16)
            query = projected[:, 0]
            key_new = projected[:, 1]
            val_new = projected[:, 2]
            new_keys.append(key_new)
            new_vals.append(val_new)
            if layer == layer_count - 1 and layer > 0:
                partial_value = attend_gathered(
                    query, key_new, val_new, suffix_cache[layer], last_prompt, valid,
                    group_id, prompt_owner, w_out[layer],
                )
            elif layer == 0:
                gathered = spread(payload_of(query, group_id), n_req)
            else:
                gathered = spread(payload_of(query, group_id), n_req)
            if layer < layer_count - 1 or layer == 0:
              partial_value = attend_project(
                gathered,
                query,
                key_new,
                val_new,
                suffix_cache[layer],
                prompt_cache[layer],
                valid,
                page_group,
                n_req,
                w_out[layer],
            )
            residual = residual + head_sum(partial_value, n_head)
            normed = root_norm(residual, gain_mlp[layer]).astype(jnp.bfloat16)
            hidden_units = jax.nn.silu(
                jnp.einsum("rd,fd->rf", normed, w_up[layer], preferred_element_type=jnp.float32)
            ).astype(jnp.bfloat16)
            partial_value = jnp.dot(hidden_units, w_down[layer], preferred_element_type=jnp.float32)
            residual = residual + head_sum(partial_value, n_head)
            if layer + 1 < layer_count:
                normed = root_norm(residual, gain_attn[layer + 1]).astype(jnp.bfloat16)
        hidden = residual.astype(jnp.bfloat16)
        new_cache = jnp.stack([jnp.stack(new_keys), jnp.stack(new_vals)], axis=1)
        return (hidden, new_cache)

    return local


def solution(mesh):
    placed = (
        P("req", None),
        P(None, None, "head", None),
        P(None, "head", None),
        P(None, "head", None),
        P(None, "head", None),
        P(),
        P(),
        P(None, None, "req", "head", None),
        P(None, None, "req", "head", None),
        P("req", None),
        P(),
        P("req"),
        P("req"),
    )
    return jax.shard_map(
        make_local(mesh.shape["req"], mesh.shape["head"]),
        mesh=mesh,
        in_specs=placed,
        out_specs=(P("req", None), P(None, None, "req", "head")),
        check_vma=False,
    )
```

```python
import math

import jax
import jax.numpy as jnp
from jax import lax
from jax.experimental import pallas as pl
from jax.experimental.pallas import tpu as pltpu
from jax.sharding import PartitionSpec as P

HD = 80
PPAGES = 4


NEG_FLOOR = -1e30


def root_norm(values, gains):
    factor = lax.rsqrt(jnp.mean(values * values, axis=-1, keepdims=True) + 1e-06)
    return values * factor * gains


def head_sum(value, count):
    chips = count // 2
    value = value + lax.ppermute(value, "head", [(i, i ^ 1) for i in range(count)])

    def from_chip(shift):
        pairs = [(i, ((i // 2 + shift) % chips) * 2 + i % 2) for i in range(count)]
        return lax.ppermute(value, "head", pairs)

    later = from_chip(1)
    opposite = from_chip(2)
    earlier = from_chip(chips - 1)
    return (value + opposite) + (later + earlier)


def spread(value, count):
    copies = jnp.broadcast_to(value[None], (count,) + value.shape)
    return lax.all_to_all(copies, "req", 0, 0, tiled=True)


def send_home(parts, count):
    return lax.all_to_all(parts, "req", 0, 0, tiled=True)


def softmax_part(scores, mask, values_fn, axes):
    top = jnp.max(jnp.where(mask, scores, NEG_FLOOR), axis=axes)
    expand = top.reshape(top.shape + (1,) * len(axes))
    weights = jnp.exp(jnp.where(mask, scores - expand, NEG_FLOOR))
    total = jnp.sum(weights, axis=axes)
    mixed = values_fn(weights.astype(jnp.bfloat16))
    return top, total, mixed


def pack_part(mixed, top, total, lanes):
    pad = jnp.zeros(mixed.shape[:-1] + (lanes - HD - 2,), jnp.float32)
    return jnp.concatenate([mixed, top[..., None], total[..., None], pad], axis=-1)


def merge_kernel(back_ref, here_ref, w_ref, out_ref):
    head_count = here_ref.shape[0]
    acc = jnp.zeros(out_ref.shape, jnp.float32)
    for h in range(head_count):
        back = back_ref[:, h]
        here = here_ref[h]
        b_top = back[:, :, HD : HD + 1]
        h_top = here[:, HD : HD + 1]
        top = jnp.maximum(jnp.max(b_top, axis=0), h_top)
        b_factor = jnp.exp(b_top - top[None])
        h_factor = jnp.exp(h_top - top)
        total = jnp.sum(back[:, :, HD + 1 : HD + 2] * b_factor, axis=0) + here[:, HD + 1 : HD + 2] * h_factor
        mixed = jnp.sum(back[:, :, :HD] * b_factor, axis=0) + here[:, :HD] * h_factor
        attended = (mixed / total).astype(jnp.bfloat16)
        acc = acc + jnp.dot(attended, w_ref[h * HD : (h + 1) * HD, :], preferred_element_type=jnp.float32)
    out_ref[...] = acc


def merge_project(back, here, w_layer):
    n_src, head_count, rows, lanes = back.shape
    width = w_layer.shape[1]
    return pl.pallas_call(
        merge_kernel,
        out_shape=jax.ShapeDtypeStruct((rows, width), jnp.float32),
        in_specs=[
            pl.BlockSpec(memory_space=pltpu.VMEM),
            pl.BlockSpec(memory_space=pltpu.VMEM),
            pl.BlockSpec(memory_space=pltpu.VMEM),
        ],
        out_specs=pl.BlockSpec(memory_space=pltpu.VMEM),
    )(back, here, w_layer)


def local_part(query_heads, key_new, val_new, layer_suffix, valid, lanes):
    row_count, head_count, _ = query_heads.shape
    scale = 1.0 / math.sqrt(HD)
    page_len = layer_suffix.shape[3]
    key_heads = key_new.reshape(row_count, head_count, HD)
    val_heads = val_new.reshape(row_count, head_count, HD)
    pool = layer_suffix.shape[1]
    s_keys = layer_suffix[0].reshape(pool, head_count, HD, page_len)
    s_vals = layer_suffix[1].reshape(pool, head_count, HD, page_len)
    s_scores = (
        jnp.einsum("ihd,phdt->ihpt", query_heads, s_keys, preferred_element_type=jnp.float32)
        * scale
    )
    s_top, s_total, s_mixed = softmax_part(
        s_scores,
        valid[:, None],
        lambda w: jnp.einsum("ihpt,phdt->ihd", w, s_vals, preferred_element_type=jnp.float32),
        (2, 3),
    )
    own = (
        jnp.einsum("rhd,rhd->rh", query_heads, key_heads, preferred_element_type=jnp.float32)
        * scale
    )
    l_top = jnp.maximum(s_top, own)
    s_factor = jnp.exp(s_top - l_top)
    own_weight = jnp.exp(own - l_top)
    l_total = s_total * s_factor + own_weight
    l_mixed = (
        s_mixed * s_factor[..., None]
        + own_weight.astype(jnp.bfloat16).astype(jnp.float32)[..., None]
        * val_heads.astype(jnp.float32)
    )
    return pack_part(l_mixed, l_top, l_total, lanes).transpose(1, 0, 2)


def page_kernel(q_ref, pg_ref, kv_ref, out_ref):
    n_src, rows, cols = q_ref.shape
    width = kv_ref.shape[2]
    head_count = width // HD
    pages = kv_ref.shape[1]
    scale = 1.0 / math.sqrt(HD)
    q = q_ref[:, :, 0:width].astype(jnp.float32).reshape(n_src * rows, width)
    group = q_ref[:, :, width : width + 1].astype(jnp.float32).reshape(n_src * rows, 1)
    lane = lax.broadcasted_iota(jnp.int32, q.shape, 1)
    out_ref[...] = jnp.zeros(out_ref.shape, jnp.float32)
    for h in range(head_count):
        inside = (lane >= h * HD) & (lane < (h + 1) * HD)
        q_head = jnp.where(inside, q, 0.0).astype(jnp.bfloat16)
        scores = []
        masks = []
        top = jnp.full((n_src * rows, 1), NEG_FLOOR, jnp.float32)
        for k in range(pages):
            score = jnp.dot(q_head, kv_ref[0, k], preferred_element_type=jnp.float32) * scale
            mask = group == pg_ref[0:1, k : k + 1]
            top = jnp.maximum(top, jnp.max(jnp.where(mask, score, NEG_FLOOR), axis=1, keepdims=True))
            scores.append(score)
            masks.append(mask)
        total = jnp.zeros((n_src * rows, 1), jnp.float32)
        mixed = jnp.zeros((n_src * rows, HD), jnp.float32)
        for k in range(pages):
            weight = jnp.exp(jnp.where(masks[k], scores[k] - top, NEG_FLOOR))
            total = total + jnp.sum(weight, axis=1, keepdims=True)
            mixed = mixed + lax.dot_general(
                weight.astype(jnp.bfloat16),
                kv_ref[1, k, h * HD : (h + 1) * HD, :],
                (((1,), (1,)), ((), ())),
                preferred_element_type=jnp.float32,
            )
        out_ref[:, h, :, 0:HD] = mixed.reshape(n_src, rows, HD)
        out_ref[:, h, :, HD : HD + 1] = top.reshape(n_src, rows, 1)
        out_ref[:, h, :, HD + 1 : HD + 2] = total.reshape(n_src, rows, 1)


def page_partials(payload, page_group, layer_prompt, lanes):
    n_src, rows, _ = payload.shape
    width = layer_prompt.shape[2]
    groups = jnp.zeros((8, lanes), jnp.float32).at[0, : page_group.shape[0]].set(page_group.astype(jnp.float32))
    return pl.pallas_call(
        page_kernel,
        out_shape=jax.ShapeDtypeStruct((n_src, width // HD, rows, lanes), jnp.float32),
        in_specs=[pl.BlockSpec(memory_space=pltpu.VMEM)] * 3,
        out_specs=pl.BlockSpec(memory_space=pltpu.VMEM),
    )(payload, groups, layer_prompt)


def attend_project(payload, query, key_new, val_new, layer_suffix, layer_prompt, valid, page_group, n_req, w_layer):
    row_count = query.shape[0]
    head_count = query.shape[1] // HD
    scale = 1.0 / math.sqrt(HD)
    page_len = layer_suffix.shape[3]
    lanes = 128
    query_heads = query.reshape(row_count, head_count, HD)
    key_heads = key_new.reshape(row_count, head_count, HD)
    val_heads = val_new.reshape(row_count, head_count, HD)

    here = local_part(query_heads, key_new, val_new, layer_suffix, valid, lanes)

    packed = page_partials(payload, page_group, layer_prompt, lanes)
    back = send_home(packed, n_req)
    return merge_project(back, here, w_layer)


def attend_gathered(query, key_new, val_new, layer_suffix, gathered_prompt, valid, group_id, prompt_owner, w_layer):
    row_count = query.shape[0]
    head_count = query.shape[1] // HD
    scale = 1.0 / math.sqrt(HD)
    page_len = layer_suffix.shape[3]
    lanes = 128
    query_heads = query.reshape(row_count, head_count, HD)
    here = local_part(query_heads, key_new, val_new, layer_suffix, valid, lanes)
    width = query.shape[1]
    lane_head = jnp.arange(width, dtype=jnp.int32) // HD
    heads = jnp.arange(head_count, dtype=jnp.int32)
    inside = lane_head[None, :] == heads[:, None]
    q_masked = jnp.where(inside[:, None, :], query[None], jnp.zeros((), query.dtype))
    p_scores = (
        jnp.einsum("hif,kft->hikt", q_masked, gathered_prompt[0], preferred_element_type=jnp.float32)
        * scale
    )
    match = (group_id[:, None] == (prompt_owner // PPAGES)[None, :])[None, :, :, None]
    p_top, p_total, p_wide = softmax_part(
        p_scores,
        match,
        lambda w: jnp.einsum("hikt,kft->hif", w, gathered_prompt[1], preferred_element_type=jnp.float32),
        (2, 3),
    )
    p_mixed = jnp.sum(jnp.where(inside[:, None, :], p_wide, 0.0).reshape(head_count, row_count, head_count, HD), axis=2)
    back = pack_part(p_mixed, p_top, p_total, lanes)[None]
    return merge_project(back, here, w_layer)


def payload_of(query, group_id):
    return jnp.concatenate([query, group_id.astype(jnp.bfloat16)[:, None]], axis=1)


def make_local(n_req, n_head):
    def local(
        tokens,
        w_qkv,
        w_out,
        w_up,
        w_down,
        gain_attn,
        gain_mlp,
        suffix_cache,
        prompt_cache,
        suffix_table,
        prompt_owner,
        suffix_len,
        group_id,
    ):
        row_count = tokens.shape[0]
        layer_count = w_qkv.shape[0]
        width_here = w_qkv.shape[2]
        model_width = w_qkv.shape[3]
        page_len = suffix_cache.shape[4]
        pool = suffix_cache.shape[2]
        own_pages = suffix_table.shape[1] // row_count
        prompt_here = prompt_cache.shape[2]

        table = suffix_table[0].reshape(row_count, own_pages)
        rows = jnp.arange(page_len, dtype=jnp.int32)
        page_ids = jnp.arange(pool, dtype=jnp.int32)
        valid = jnp.zeros((row_count, pool, page_len), dtype=bool)
        for slot in range(own_pages):
            chosen = (table[:, slot][:, None] == page_ids[None, :])[:, :, None]
            filled = (slot * page_len + rows)[None, None, :] < suffix_len[:, None, None]
            valid = valid | (chosen & filled)

        here = lax.axis_index("req")
        page_group = lax.dynamic_slice(prompt_owner, (here * prompt_here,), (prompt_here,)) // PPAGES

        last_prompt = lax.all_gather(prompt_cache[layer_count - 1], "req", axis=1, tiled=True)
        whole = tokens.astype(jnp.float32)
        normed = root_norm(whole, gain_attn[0]).astype(jnp.bfloat16)
        residual = whole
        new_keys = []
        new_vals = []
        for layer in range(layer_count):
            projected = jnp.einsum(
                "rd,kd->rk",
                normed,
                w_qkv[layer].reshape(3 * width_here, model_width),
                preferred_element_type=jnp.float32,
            )
            projected = projected.reshape(row_count, 3, width_here).astype(jnp.bfloat16)
            query = projected[:, 0]
            key_new = projected[:, 1]
            val_new = projected[:, 2]
            new_keys.append(key_new)
            new_vals.append(val_new)
            if layer == layer_count - 1 and layer > 0:
                partial_value = attend_gathered(
                    query, key_new, val_new, suffix_cache[layer], last_prompt, valid,
                    group_id, prompt_owner, w_out[layer],
                )
            elif layer == 0:
                gathered = spread(payload_of(query, group_id), n_req)
            else:
                gathered = spread(payload_of(query, group_id), n_req)
            if layer < layer_count - 1 or layer == 0:
              partial_value = attend_project(
                gathered,
                query,
                key_new,
                val_new,
                suffix_cache[layer],
                prompt_cache[layer],
                valid,
                page_group,
                n_req,
                w_out[layer],
            )
            residual = residual + head_sum(partial_value, n_head)
            normed = root_norm(residual, gain_mlp[layer]).astype(jnp.bfloat16)
            hidden_units = jax.nn.silu(
                jnp.einsum("rd,fd->rf", normed, w_up[layer], preferred_element_type=jnp.float32)
            ).astype(jnp.bfloat16)
            partial_value = jnp.dot(hidden_units, w_down[layer], preferred_element_type=jnp.float32)
            residual = residual + head_sum(partial_value, n_head)
            if layer + 1 < layer_count:
                normed = root_norm(residual, gain_attn[layer + 1]).astype(jnp.bfloat16)
        hidden = residual.astype(jnp.bfloat16)
        new_cache = jnp.stack([jnp.stack(new_keys), jnp.stack(new_vals)], axis=1)
        return (hidden, new_cache)

    return local


def solution(mesh):
    placed = (
        P("req", None),
        P(None, None, "head", None),
        P(None, "head", None),
        P(None, "head", None),
        P(None, "head", None),
        P(),
        P(),
        P(None, None, "req", "head", None),
        P(None, None, "req", "head", None),
        P("req", None),
        P(),
        P("req"),
        P("req"),
    )
    return jax.shard_map(
        make_local(mesh.shape["req"], mesh.shape["head"]),
        mesh=mesh,
        in_specs=placed,
        out_specs=(P("req", None), P(None, None, "req", "head")),
        check_vma=False,
    )
```

```python
import math

import jax
import jax.numpy as jnp
from jax import lax
from jax.experimental import pallas as pl
from jax.experimental.pallas import tpu as pltpu
from jax.sharding import PartitionSpec as P

HD = 80
PPAGES = 4


NEG_FLOOR = -1e30


def root_norm(values, gains):
    factor = lax.rsqrt(jnp.mean(values * values, axis=-1, keepdims=True) + 1e-06)
    return values * factor * gains


def head_sum(value, count):
    chips = count // 2
    value = value + lax.ppermute(value, "head", [(i, i ^ 1) for i in range(count)])

    def from_chip(shift):
        pairs = [(i, ((i // 2 + shift) % chips) * 2 + i % 2) for i in range(count)]
        return lax.ppermute(value, "head", pairs)

    later = from_chip(1)
    opposite = from_chip(2)
    earlier = from_chip(chips - 1)
    return (value + opposite) + (later + earlier)


def spread(value, count):
    copies = jnp.broadcast_to(value[None], (count,) + value.shape)
    return lax.all_to_all(copies, "req", 0, 0, tiled=True)


def send_home(parts, count):
    return lax.all_to_all(parts, "req", 0, 0, tiled=True)


def softmax_part(scores, mask, values_fn, axes):
    top = jnp.max(jnp.where(mask, scores, NEG_FLOOR), axis=axes)
    expand = top.reshape(top.shape + (1,) * len(axes))
    weights = jnp.exp(jnp.where(mask, scores - expand, NEG_FLOOR))
    total = jnp.sum(weights, axis=axes)
    mixed = values_fn(weights.astype(jnp.bfloat16))
    return top, total, mixed


def pack_part(mixed, top, total, lanes):
    pad = jnp.zeros(mixed.shape[:-1] + (lanes - HD - 2,), jnp.float32)
    return jnp.concatenate([mixed, top[..., None], total[..., None], pad], axis=-1)


def merge_kernel(back_ref, here_ref, w_ref, out_ref):
    head_count = here_ref.shape[0]
    acc = jnp.zeros(out_ref.shape, jnp.float32)
    for h in range(head_count):
        back = back_ref[:, h]
        here = here_ref[h]
        b_top = back[:, :, HD : HD + 1]
        h_top = here[:, HD : HD + 1]
        top = jnp.maximum(jnp.max(b_top, axis=0), h_top)
        b_factor = jnp.exp(b_top - top[None])
        h_factor = jnp.exp(h_top - top)
        total = jnp.sum(back[:, :, HD + 1 : HD + 2] * b_factor, axis=0) + here[:, HD + 1 : HD + 2] * h_factor
        mixed = jnp.sum(back[:, :, :HD] * b_factor, axis=0) + here[:, :HD] * h_factor
        attended = (mixed / total).astype(jnp.bfloat16)
        acc = acc + jnp.dot(attended, w_ref[h * HD : (h + 1) * HD, :], preferred_element_type=jnp.float32)
    out_ref[...] = acc


def merge_project(back, here, w_layer):
    n_src, head_count, rows, lanes = back.shape
    width = w_layer.shape[1]
    return pl.pallas_call(
        merge_kernel,
        out_shape=jax.ShapeDtypeStruct((rows, width), jnp.float32),
        in_specs=[
            pl.BlockSpec(memory_space=pltpu.VMEM),
            pl.BlockSpec(memory_space=pltpu.VMEM),
            pl.BlockSpec(memory_space=pltpu.VMEM),
        ],
        out_specs=pl.BlockSpec(memory_space=pltpu.VMEM),
    )(back, here, w_layer)


def masked_queries(query, head_count):
    width = query.shape[1]
    lane_head = jnp.arange(width, dtype=jnp.int32) // HD
    inside = lane_head[None, :] == jnp.arange(head_count, dtype=jnp.int32)[:, None]
    return jnp.where(inside[:, None, :], query[None], jnp.zeros((), query.dtype)), inside


def own_head_features(wide, inside):
    head_count, row_count, _ = wide.shape
    picked = jnp.where(inside[:, None, :], wide, 0.0).reshape(head_count, row_count, head_count, HD)
    return jnp.sum(picked, axis=2)


def local_part(query_heads, key_new, val_new, layer_suffix, valid, lanes):
    row_count, head_count, _ = query_heads.shape
    scale = 1.0 / math.sqrt(HD)
    page_len = layer_suffix.shape[3]
    key_heads = key_new.reshape(row_count, head_count, HD)
    val_heads = val_new.reshape(row_count, head_count, HD)
    query = query_heads.reshape(row_count, head_count * HD)
    q_masked, inside = masked_queries(query, head_count)
    s_scores = (
        jnp.einsum("hif,pft->hipt", q_masked, layer_suffix[0], preferred_element_type=jnp.float32)
        * scale
    )
    s_top, s_total, s_wide = softmax_part(
        s_scores,
        valid[None],
        lambda w: jnp.einsum("hipt,pft->hif", w, layer_suffix[1], preferred_element_type=jnp.float32),
        (2, 3),
    )
    s_mixed = own_head_features(s_wide, inside).transpose(1, 0, 2)
    s_top = s_top.T
    s_total = s_total.T
    own = (
        jnp.einsum("rhd,rhd->rh", query_heads, key_heads, preferred_element_type=jnp.float32)
        * scale
    )
    l_top = jnp.maximum(s_top, own)
    s_factor = jnp.exp(s_top - l_top)
    own_weight = jnp.exp(own - l_top)
    l_total = s_total * s_factor + own_weight
    l_mixed = (
        s_mixed * s_factor[..., None]
        + own_weight.astype(jnp.bfloat16).astype(jnp.float32)[..., None]
        * val_heads.astype(jnp.float32)
    )
    return pack_part(l_mixed, l_top, l_total, lanes).transpose(1, 0, 2)


def page_kernel(q_ref, pg_ref, kv_ref, out_ref):
    n_src, rows, cols = q_ref.shape
    width = kv_ref.shape[2]
    head_count = width // HD
    pages = kv_ref.shape[1]
    scale = 1.0 / math.sqrt(HD)
    q = q_ref[:, :, 0:width].astype(jnp.float32).reshape(n_src * rows, width)
    group = q_ref[:, :, width : width + 1].astype(jnp.float32).reshape(n_src * rows, 1)
    lane = lax.broadcasted_iota(jnp.int32, q.shape, 1)
    out_ref[...] = jnp.zeros(out_ref.shape, jnp.float32)
    for h in range(head_count):
        inside = (lane >= h * HD) & (lane < (h + 1) * HD)
        q_head = jnp.where(inside, q, 0.0).astype(jnp.bfloat16)
        scores = []
        masks = []
        top = jnp.full((n_src * rows, 1), NEG_FLOOR, jnp.float32)
        for k in range(pages):
            score = jnp.dot(q_head, kv_ref[0, k], preferred_element_type=jnp.float32) * scale
            mask = group == pg_ref[0:1, k : k + 1]
            top = jnp.maximum(top, jnp.max(jnp.where(mask, score, NEG_FLOOR), axis=1, keepdims=True))
            scores.append(score)
            masks.append(mask)
        total = jnp.zeros((n_src * rows, 1), jnp.float32)
        mixed = jnp.zeros((n_src * rows, HD), jnp.float32)
        for k in range(pages):
            weight = jnp.exp(jnp.where(masks[k], scores[k] - top, NEG_FLOOR))
            total = total + jnp.sum(weight, axis=1, keepdims=True)
            mixed = mixed + lax.dot_general(
                weight.astype(jnp.bfloat16),
                kv_ref[1, k, h * HD : (h + 1) * HD, :],
                (((1,), (1,)), ((), ())),
                preferred_element_type=jnp.float32,
            )
        out_ref[:, h, :, 0:HD] = mixed.reshape(n_src, rows, HD)
        out_ref[:, h, :, HD : HD + 1] = top.reshape(n_src, rows, 1)
        out_ref[:, h, :, HD + 1 : HD + 2] = total.reshape(n_src, rows, 1)


def page_partials(payload, page_group, layer_prompt, lanes):
    n_src, rows, _ = payload.shape
    width = layer_prompt.shape[2]
    groups = jnp.zeros((8, lanes), jnp.float32).at[0, : page_group.shape[0]].set(page_group.astype(jnp.float32))
    return pl.pallas_call(
        page_kernel,
        out_shape=jax.ShapeDtypeStruct((n_src, width // HD, rows, lanes), jnp.float32),
        in_specs=[pl.BlockSpec(memory_space=pltpu.VMEM)] * 3,
        out_specs=pl.BlockSpec(memory_space=pltpu.VMEM),
    )(payload, groups, layer_prompt)


def attend_project(payload, query, key_new, val_new, layer_suffix, layer_prompt, valid, page_group, n_req, w_layer):
    row_count = query.shape[0]
    head_count = query.shape[1] // HD
    scale = 1.0 / math.sqrt(HD)
    page_len = layer_suffix.shape[3]
    lanes = 128
    query_heads = query.reshape(row_count, head_count, HD)
    key_heads = key_new.reshape(row_count, head_count, HD)
    val_heads = val_new.reshape(row_count, head_count, HD)

    here = local_part(query_heads, key_new, val_new, layer_suffix, valid, lanes)

    packed = page_partials(payload, page_group, layer_prompt, lanes)
    back = send_home(packed, n_req)
    return merge_project(back, here, w_layer)


def attend_gathered(query, key_new, val_new, layer_suffix, gathered_prompt, valid, group_id, prompt_owner, w_layer):
    row_count = query.shape[0]
    head_count = query.shape[1] // HD
    scale = 1.0 / math.sqrt(HD)
    page_len = layer_suffix.shape[3]
    lanes = 128
    query_heads = query.reshape(row_count, head_count, HD)
    here = local_part(query_heads, key_new, val_new, layer_suffix, valid, lanes)
    q_masked, inside = masked_queries(query, head_count)
    p_scores = (
        jnp.einsum("hif,kft->hikt", q_masked, gathered_prompt[0], preferred_element_type=jnp.float32)
        * scale
    )
    match = (group_id[:, None] == (prompt_owner // PPAGES)[None, :])[None, :, :, None]
    p_top, p_total, p_wide = softmax_part(
        p_scores,
        match,
        lambda w: jnp.einsum("hikt,kft->hif", w, gathered_prompt[1], preferred_element_type=jnp.float32),
        (2, 3),
    )
    p_mixed = own_head_features(p_wide, inside)
    back = pack_part(p_mixed, p_top, p_total, lanes)[None]
    return merge_project(back, here, w_layer)


def payload_of(query, group_id):
    return jnp.concatenate([query, group_id.astype(jnp.bfloat16)[:, None]], axis=1)


def make_local(n_req, n_head):
    def local(
        tokens,
        w_qkv,
        w_out,
        w_up,
        w_down,
        gain_attn,
        gain_mlp,
        suffix_cache,
        prompt_cache,
        suffix_table,
        prompt_owner,
        suffix_len,
        group_id,
    ):
        row_count = tokens.shape[0]
        layer_count = w_qkv.shape[0]
        width_here = w_qkv.shape[2]
        model_width = w_qkv.shape[3]
        page_len = suffix_cache.shape[4]
        pool = suffix_cache.shape[2]
        own_pages = suffix_table.shape[1] // row_count
        prompt_here = prompt_cache.shape[2]

        table = suffix_table[0].reshape(row_count, own_pages)
        rows = jnp.arange(page_len, dtype=jnp.int32)
        page_ids = jnp.arange(pool, dtype=jnp.int32)
        valid = jnp.zeros((row_count, pool, page_len), dtype=bool)
        for slot in range(own_pages):
            chosen = (table[:, slot][:, None] == page_ids[None, :])[:, :, None]
            filled = (slot * page_len + rows)[None, None, :] < suffix_len[:, None, None]
            valid = valid | (chosen & filled)

        here = lax.axis_index("req")
        page_group = lax.dynamic_slice(prompt_owner, (here * prompt_here,), (prompt_here,)) // PPAGES

        last_prompt = lax.all_gather(prompt_cache[layer_count - 1], "req", axis=1, tiled=True)
        whole = tokens.astype(jnp.float32)
        normed = root_norm(whole, gain_attn[0]).astype(jnp.bfloat16)
        residual = whole
        new_keys = []
        new_vals = []
        for layer in range(layer_count):
            projected = jnp.einsum(
                "rd,kd->rk",
                normed,
                w_qkv[layer].reshape(3 * width_here, model_width),
                preferred_element_type=jnp.float32,
            )
            projected = projected.reshape(row_count, 3, width_here).astype(jnp.bfloat16)
            query = projected[:, 0]
            key_new = projected[:, 1]
            val_new = projected[:, 2]
            new_keys.append(key_new)
            new_vals.append(val_new)
            if layer == layer_count - 1 and layer > 0:
                partial_value = attend_gathered(
                    query, key_new, val_new, suffix_cache[layer], last_prompt, valid,
                    group_id, prompt_owner, w_out[layer],
                )
            elif layer == 0:
                gathered = spread(payload_of(query, group_id), n_req)
            else:
                gathered = spread(payload_of(query, group_id), n_req)
            if layer < layer_count - 1 or layer == 0:
              partial_value = attend_project(
                gathered,
                query,
                key_new,
                val_new,
                suffix_cache[layer],
                prompt_cache[layer],
                valid,
                page_group,
                n_req,
                w_out[layer],
            )
            residual = residual + head_sum(partial_value, n_head)
            normed = root_norm(residual, gain_mlp[layer]).astype(jnp.bfloat16)
            hidden_units = jax.nn.silu(
                jnp.einsum("rd,fd->rf", normed, w_up[layer], preferred_element_type=jnp.float32)
            ).astype(jnp.bfloat16)
            partial_value = jnp.dot(hidden_units, w_down[layer], preferred_element_type=jnp.float32)
            residual = residual + head_sum(partial_value, n_head)
            if layer + 1 < layer_count:
                normed = root_norm(residual, gain_attn[layer + 1]).astype(jnp.bfloat16)
        hidden = residual.astype(jnp.bfloat16)
        new_cache = jnp.stack([jnp.stack(new_keys), jnp.stack(new_vals)], axis=1)
        return (hidden, new_cache)

    return local


def solution(mesh):
    placed = (
        P("req", None),
        P(None, None, "head", None),
        P(None, "head", None),
        P(None, "head", None),
        P(None, "head", None),
        P(),
        P(),
        P(None, None, "req", "head", None),
        P(None, None, "req", "head", None),
        P("req", None),
        P(),
        P("req"),
        P("req"),
    )
    return jax.shard_map(
        make_local(mesh.shape["req"], mesh.shape["head"]),
        mesh=mesh,
        in_specs=placed,
        out_specs=(P("req", None), P(None, None, "req", "head")),
        check_vma=False,
    )
```

```python
import math

import jax
import jax.numpy as jnp
from jax import lax
from jax.experimental import pallas as pl
from jax.experimental.pallas import tpu as pltpu
from jax.sharding import PartitionSpec as P

HD = 80
PPAGES = 4


NEG_FLOOR = -1e30


def root_norm(values, gains):
    factor = lax.rsqrt(jnp.mean(values * values, axis=-1, keepdims=True) + 1e-06)
    return values * factor * gains


def head_sum(value, count):
    chips = count // 2
    value = value + lax.ppermute(value, "head", [(i, i ^ 1) for i in range(count)])

    def from_chip(shift):
        pairs = [(i, ((i // 2 + shift) % chips) * 2 + i % 2) for i in range(count)]
        return lax.ppermute(value, "head", pairs)

    later = from_chip(1)
    opposite = from_chip(2)
    earlier = from_chip(chips - 1)
    return (value + opposite) + (later + earlier)


def spread(value, count):
    copies = jnp.broadcast_to(value[None], (count,) + value.shape)
    return lax.all_to_all(copies, "req", 0, 0, tiled=True)


def send_home(parts, count):
    return lax.all_to_all(parts, "req", 0, 0, tiled=True)


def softmax_part(scores, mask, values_fn, axes):
    top = jnp.max(jnp.where(mask, scores, NEG_FLOOR), axis=axes)
    expand = top.reshape(top.shape + (1,) * len(axes))
    weights = jnp.exp(jnp.where(mask, scores - expand, NEG_FLOOR))
    total = jnp.sum(weights, axis=axes)
    mixed = values_fn(weights.astype(jnp.bfloat16))
    return top, total, mixed


def pack_part(mixed, top, total, lanes):
    pad = jnp.zeros(mixed.shape[:-1] + (lanes - HD - 2,), jnp.float32)
    return jnp.concatenate([mixed, top[..., None], total[..., None], pad], axis=-1)


def merge_kernel(back_ref, here_ref, w_ref, out_ref):
    head_count = here_ref.shape[0]
    acc = jnp.zeros(out_ref.shape, jnp.float32)
    for h in range(head_count):
        back = back_ref[:, h]
        here = here_ref[h]
        b_top = back[:, :, HD : HD + 1]
        h_top = here[:, HD : HD + 1]
        top = jnp.maximum(jnp.max(b_top, axis=0), h_top)
        b_factor = jnp.exp(b_top - top[None])
        h_factor = jnp.exp(h_top - top)
        total = jnp.sum(back[:, :, HD + 1 : HD + 2] * b_factor, axis=0) + here[:, HD + 1 : HD + 2] * h_factor
        mixed = jnp.sum(back[:, :, :HD] * b_factor, axis=0) + here[:, :HD] * h_factor
        attended = (mixed / total).astype(jnp.bfloat16)
        acc = acc + jnp.dot(attended, w_ref[h * HD : (h + 1) * HD, :], preferred_element_type=jnp.float32)
    out_ref[...] = acc


def merge_project(back, here, w_layer):
    n_src, head_count, rows, lanes = back.shape
    width = w_layer.shape[1]
    return pl.pallas_call(
        merge_kernel,
        out_shape=jax.ShapeDtypeStruct((rows, width), jnp.float32),
        in_specs=[
            pl.BlockSpec(memory_space=pltpu.VMEM),
            pl.BlockSpec(memory_space=pltpu.VMEM),
            pl.BlockSpec(memory_space=pltpu.VMEM),
        ],
        out_specs=pl.BlockSpec(memory_space=pltpu.VMEM),
    )(back, here, w_layer)


def local_part(query_heads, key_new, val_new, layer_suffix, valid, lanes):
    row_count, head_count, _ = query_heads.shape
    scale = 1.0 / math.sqrt(HD)
    page_len = layer_suffix.shape[3]
    key_heads = key_new.reshape(row_count, head_count, HD)
    val_heads = val_new.reshape(row_count, head_count, HD)
    pool = layer_suffix.shape[1]
    s_keys = layer_suffix[0].reshape(pool, head_count, HD, page_len)
    s_vals = layer_suffix[1].reshape(pool, head_count, HD, page_len)
    s_scores = (
        jnp.einsum("ihd,phdt->ihpt", query_heads, s_keys, preferred_element_type=jnp.float32)
        * scale
    )
    s_top, s_total, s_mixed = softmax_part(
        s_scores,
        valid[:, None],
        lambda w: jnp.einsum("ihpt,phdt->ihd", w, s_vals, preferred_element_type=jnp.float32),
        (2, 3),
    )
    own = (
        jnp.einsum("rhd,rhd->rh", query_heads, key_heads, preferred_element_type=jnp.float32)
        * scale
    )
    l_top = jnp.maximum(s_top, own)
    s_factor = jnp.exp(s_top - l_top)
    own_weight = jnp.exp(own - l_top)
    l_total = s_total * s_factor + own_weight
    l_mixed = (
        s_mixed * s_factor[..., None]
        + own_weight.astype(jnp.bfloat16).astype(jnp.float32)[..., None]
        * val_heads.astype(jnp.float32)
    )
    return pack_part(l_mixed, l_top, l_total, lanes).transpose(1, 0, 2)


def page_kernel(q_ref, pg_ref, kv_ref, out_ref):
    n_src, rows, cols = q_ref.shape
    width = kv_ref.shape[2]
    head_count = width // HD
    pages = kv_ref.shape[1]
    scale = 1.0 / math.sqrt(HD)
    q = q_ref[:, :, 0:width].astype(jnp.float32).reshape(n_src * rows, width)
    group = q_ref[:, :, width : width + 1].astype(jnp.float32).reshape(n_src * rows, 1)
    lane = lax.broadcasted_iota(jnp.int32, q.shape, 1)
    out_ref[...] = jnp.zeros(out_ref.shape, jnp.float32)
    for h in range(head_count):
        inside = (lane >= h * HD) & (lane < (h + 1) * HD)
        q_head = jnp.where(inside, q, 0.0).astype(jnp.bfloat16)
        scores = []
        masks = []
        top = jnp.full((n_src * rows, 1), NEG_FLOOR, jnp.float32)
        for k in range(pages):
            score = jnp.dot(q_head, kv_ref[0, k], preferred_element_type=jnp.float32) * scale
            mask = group == pg_ref[0:1, k : k + 1]
            top = jnp.maximum(top, jnp.max(jnp.where(mask, score, NEG_FLOOR), axis=1, keepdims=True))
            scores.append(score)
            masks.append(mask)
        total = jnp.zeros((n_src * rows, 1), jnp.float32)
        mixed = jnp.zeros((n_src * rows, HD), jnp.float32)
        for k in range(pages):
            weight = jnp.exp(jnp.where(masks[k], scores[k] - top, NEG_FLOOR))
            total = total + jnp.sum(weight, axis=1, keepdims=True)
            mixed = mixed + lax.dot_general(
                weight.astype(jnp.bfloat16),
                kv_ref[1, k, h * HD : (h + 1) * HD, :],
                (((1,), (1,)), ((), ())),
                preferred_element_type=jnp.float32,
            )
        out_ref[:, h, :, 0:HD] = mixed.reshape(n_src, rows, HD)
        out_ref[:, h, :, HD : HD + 1] = top.reshape(n_src, rows, 1)
        out_ref[:, h, :, HD + 1 : HD + 2] = total.reshape(n_src, rows, 1)


def page_partials(payload, page_group, layer_prompt, lanes):
    n_src, rows, _ = payload.shape
    width = layer_prompt.shape[2]
    groups = jnp.zeros((8, lanes), jnp.float32).at[0, : page_group.shape[0]].set(page_group.astype(jnp.float32))
    return pl.pallas_call(
        page_kernel,
        out_shape=jax.ShapeDtypeStruct((n_src, width // HD, rows, lanes), jnp.float32),
        in_specs=[pl.BlockSpec(memory_space=pltpu.VMEM)] * 3,
        out_specs=pl.BlockSpec(memory_space=pltpu.VMEM),
    )(payload, groups, layer_prompt)


def attend_project(payload, query, key_new, val_new, layer_suffix, layer_prompt, valid, page_group, n_req, w_layer):
    row_count = query.shape[0]
    head_count = query.shape[1] // HD
    scale = 1.0 / math.sqrt(HD)
    page_len = layer_suffix.shape[3]
    lanes = 128
    query_heads = query.reshape(row_count, head_count, HD)
    key_heads = key_new.reshape(row_count, head_count, HD)
    val_heads = val_new.reshape(row_count, head_count, HD)

    packed = page_partials(payload, page_group, layer_prompt, lanes)
    packed, query_heads = lax.optimization_barrier((packed, query_heads))
    back = send_home(packed, n_req)
    here = local_part(query_heads, key_new, val_new, layer_suffix, valid, lanes)
    return merge_project(back, here, w_layer)


def attend_gathered(query, key_new, val_new, layer_suffix, gathered_prompt, valid, group_id, prompt_owner, w_layer):
    row_count = query.shape[0]
    head_count = query.shape[1] // HD
    scale = 1.0 / math.sqrt(HD)
    page_len = layer_suffix.shape[3]
    lanes = 128
    query_heads = query.reshape(row_count, head_count, HD)
    here = local_part(query_heads, key_new, val_new, layer_suffix, valid, lanes)
    width = query.shape[1]
    lane_head = jnp.arange(width, dtype=jnp.int32) // HD
    heads = jnp.arange(head_count, dtype=jnp.int32)
    inside = lane_head[None, :] == heads[:, None]
    q_masked = jnp.where(inside[:, None, :], query[None], jnp.zeros((), query.dtype))
    p_scores = (
        jnp.einsum("hif,kft->hikt", q_masked, gathered_prompt[0], preferred_element_type=jnp.float32)
        * scale
    )
    match = (group_id[:, None] == (prompt_owner // PPAGES)[None, :])[None, :, :, None]
    p_top, p_total, p_wide = softmax_part(
        p_scores,
        match,
        lambda w: jnp.einsum("hikt,kft->hif", w, gathered_prompt[1], preferred_element_type=jnp.float32),
        (2, 3),
    )
    p_mixed = jnp.sum(jnp.where(inside[:, None, :], p_wide, 0.0).reshape(head_count, row_count, head_count, HD), axis=2)
    back = pack_part(p_mixed, p_top, p_total, lanes)[None]
    return merge_project(back, here, w_layer)


def payload_of(query, group_id):
    return jnp.concatenate([query, group_id.astype(jnp.bfloat16)[:, None]], axis=1)


def make_local(n_req, n_head):
    def local(
        tokens,
        w_qkv,
        w_out,
        w_up,
        w_down,
        gain_attn,
        gain_mlp,
        suffix_cache,
        prompt_cache,
        suffix_table,
        prompt_owner,
        suffix_len,
        group_id,
    ):
        row_count = tokens.shape[0]
        layer_count = w_qkv.shape[0]
        width_here = w_qkv.shape[2]
        model_width = w_qkv.shape[3]
        page_len = suffix_cache.shape[4]
        pool = suffix_cache.shape[2]
        own_pages = suffix_table.shape[1] // row_count
        prompt_here = prompt_cache.shape[2]

        table = suffix_table[0].reshape(row_count, own_pages)
        rows = jnp.arange(page_len, dtype=jnp.int32)
        page_ids = jnp.arange(pool, dtype=jnp.int32)
        valid = jnp.zeros((row_count, pool, page_len), dtype=bool)
        for slot in range(own_pages):
            chosen = (table[:, slot][:, None] == page_ids[None, :])[:, :, None]
            filled = (slot * page_len + rows)[None, None, :] < suffix_len[:, None, None]
            valid = valid | (chosen & filled)

        here = lax.axis_index("req")
        page_group = lax.dynamic_slice(prompt_owner, (here * prompt_here,), (prompt_here,)) // PPAGES

        last_prompt = lax.all_gather(prompt_cache[layer_count - 1], "req", axis=1, tiled=True)
        whole = tokens.astype(jnp.float32)
        normed = root_norm(whole, gain_attn[0]).astype(jnp.bfloat16)
        residual = whole
        new_keys = []
        new_vals = []
        for layer in range(layer_count):
            projected = jnp.einsum(
                "rd,kd->rk",
                normed,
                w_qkv[layer].reshape(3 * width_here, model_width),
                preferred_element_type=jnp.float32,
            )
            projected = projected.reshape(row_count, 3, width_here).astype(jnp.bfloat16)
            query = projected[:, 0]
            key_new = projected[:, 1]
            val_new = projected[:, 2]
            new_keys.append(key_new)
            new_vals.append(val_new)
            if layer == layer_count - 1 and layer > 0:
                partial_value = attend_gathered(
                    query, key_new, val_new, suffix_cache[layer], last_prompt, valid,
                    group_id, prompt_owner, w_out[layer],
                )
            elif layer == 0:
                gathered = spread(payload_of(query, group_id), n_req)
            else:
                gathered = spread(payload_of(query, group_id), n_req)
            if layer < layer_count - 1 or layer == 0:
              partial_value = attend_project(
                gathered,
                query,
                key_new,
                val_new,
                suffix_cache[layer],
                prompt_cache[layer],
                valid,
                page_group,
                n_req,
                w_out[layer],
            )
            residual = residual + head_sum(partial_value, n_head)
            normed = root_norm(residual, gain_mlp[layer]).astype(jnp.bfloat16)
            hidden_units = jax.nn.silu(
                jnp.einsum("rd,fd->rf", normed, w_up[layer], preferred_element_type=jnp.float32)
            ).astype(jnp.bfloat16)
            partial_value = jnp.dot(hidden_units, w_down[layer], preferred_element_type=jnp.float32)
            residual = residual + head_sum(partial_value, n_head)
            if layer + 1 < layer_count:
                normed = root_norm(residual, gain_attn[layer + 1]).astype(jnp.bfloat16)
        hidden = residual.astype(jnp.bfloat16)
        new_cache = jnp.stack([jnp.stack(new_keys), jnp.stack(new_vals)], axis=1)
        return (hidden, new_cache)

    return local


def solution(mesh):
    placed = (
        P("req", None),
        P(None, None, "head", None),
        P(None, "head", None),
        P(None, "head", None),
        P(None, "head", None),
        P(),
        P(),
        P(None, None, "req", "head", None),
        P(None, None, "req", "head", None),
        P("req", None),
        P(),
        P("req"),
        P("req"),
    )
    return jax.shard_map(
        make_local(mesh.shape["req"], mesh.shape["head"]),
        mesh=mesh,
        in_specs=placed,
        out_specs=(P("req", None), P(None, None, "req", "head")),
        check_vma=False,
    )
```

```python
import math

import jax
import jax.numpy as jnp
from jax import lax
from jax.experimental import pallas as pl
from jax.experimental.pallas import tpu as pltpu
from jax.sharding import PartitionSpec as P

HD = 80
PPAGES = 4


NEG_FLOOR = -1e30


def root_norm(values, gains):
    factor = lax.rsqrt(jnp.mean(values * values, axis=-1, keepdims=True) + 1e-06)
    return values * factor * gains


def head_sum(value, count):
    chips = count // 2
    value = value + lax.ppermute(value, "head", [(i, i ^ 1) for i in range(count)])

    def from_chip(shift):
        pairs = [(i, ((i // 2 + shift) % chips) * 2 + i % 2) for i in range(count)]
        return lax.ppermute(value, "head", pairs)

    later = from_chip(1)
    opposite = from_chip(2)
    earlier = from_chip(chips - 1)
    return (value + opposite) + (later + earlier)


def spread(value, count):
    copies = jnp.broadcast_to(value[None], (count,) + value.shape)
    return lax.all_to_all(copies, "req", 0, 0, tiled=True)


def send_home(parts, count):
    return lax.all_to_all(parts, "req", 0, 0, tiled=True)


def softmax_part(scores, mask, values_fn, axes):
    top = jnp.max(jnp.where(mask, scores, NEG_FLOOR), axis=axes)
    expand = top.reshape(top.shape + (1,) * len(axes))
    weights = jnp.exp(jnp.where(mask, scores - expand, NEG_FLOOR))
    total = jnp.sum(weights, axis=axes)
    mixed = values_fn(weights.astype(jnp.bfloat16))
    return top, total, mixed


def pack_part(mixed, top, total, lanes):
    pad = jnp.zeros(mixed.shape[:-1] + (lanes - HD - 2,), jnp.float32)
    return jnp.concatenate([mixed, top[..., None], total[..., None], pad], axis=-1)


def merge_kernel(back_ref, here_ref, w_ref, out_ref):
    head_count = here_ref.shape[0]
    acc = jnp.zeros(out_ref.shape, jnp.float32)
    for h in range(head_count):
        back = back_ref[:, h]
        here = here_ref[h]
        b_top = back[:, :, HD : HD + 1]
        h_top = here[:, HD : HD + 1]
        top = jnp.maximum(jnp.max(b_top, axis=0), h_top)
        b_factor = jnp.exp(b_top - top[None])
        h_factor = jnp.exp(h_top - top)
        total = jnp.sum(back[:, :, HD + 1 : HD + 2] * b_factor, axis=0) + here[:, HD + 1 : HD + 2] * h_factor
        mixed = jnp.sum(back[:, :, :HD] * b_factor, axis=0) + here[:, :HD] * h_factor
        attended = (mixed / total).astype(jnp.bfloat16)
        acc = acc + jnp.dot(attended, w_ref[h * HD : (h + 1) * HD, :], preferred_element_type=jnp.float32)
    out_ref[...] = acc


def merge_project(back, here, w_layer):
    n_src, head_count, rows, lanes = back.shape
    width = w_layer.shape[1]
    return pl.pallas_call(
        merge_kernel,
        out_shape=jax.ShapeDtypeStruct((rows, width), jnp.float32),
        in_specs=[
            pl.BlockSpec(memory_space=pltpu.VMEM),
            pl.BlockSpec(memory_space=pltpu.VMEM),
            pl.BlockSpec(memory_space=pltpu.VMEM),
        ],
        out_specs=pl.BlockSpec(memory_space=pltpu.VMEM),
    )(back, here, w_layer)


def masked_queries(query, head_count):
    width = query.shape[1]
    lane_head = jnp.arange(width, dtype=jnp.int32) // HD
    inside = lane_head[None, :] == jnp.arange(head_count, dtype=jnp.int32)[:, None]
    return jnp.where(inside[:, None, :], query[None], jnp.zeros((), query.dtype)), inside


def own_head_features(wide, inside):
    head_count, row_count, _ = wide.shape
    picked = jnp.where(inside[:, None, :], wide, 0.0).reshape(head_count, row_count, head_count, HD)
    return jnp.sum(picked, axis=2)


def local_part(query_heads, key_new, val_new, layer_suffix, valid, lanes):
    row_count, head_count, _ = query_heads.shape
    scale = 1.0 / math.sqrt(HD)
    page_len = layer_suffix.shape[3]
    key_heads = key_new.reshape(row_count, head_count, HD)
    val_heads = val_new.reshape(row_count, head_count, HD)
    query = query_heads.reshape(row_count, head_count * HD)
    q_masked, inside = masked_queries(query, head_count)
    s_scores = (
        jnp.einsum("hif,pft->hipt", q_masked, layer_suffix[0], preferred_element_type=jnp.float32)
        * scale
    )
    s_top, s_total, s_wide = softmax_part(
        s_scores,
        valid[None],
        lambda w: jnp.einsum("hipt,pft->hif", w, layer_suffix[1], preferred_element_type=jnp.float32),
        (2, 3),
    )
    s_mixed = own_head_features(s_wide, inside).transpose(1, 0, 2)
    s_top = s_top.T
    s_total = s_total.T
    own = (
        jnp.einsum("rhd,rhd->rh", query_heads, key_heads, preferred_element_type=jnp.float32)
        * scale
    )
    l_top = jnp.maximum(s_top, own)
    s_factor = jnp.exp(s_top - l_top)
    own_weight = jnp.exp(own - l_top)
    l_total = s_total * s_factor + own_weight
    l_mixed = (
        s_mixed * s_factor[..., None]
        + own_weight.astype(jnp.bfloat16).astype(jnp.float32)[..., None]
        * val_heads.astype(jnp.float32)
    )
    return pack_part(l_mixed, l_top, l_total, lanes).transpose(1, 0, 2)


def page_kernel(q_ref, pg_ref, kv_ref, out_ref):
    n_src, rows, cols = q_ref.shape
    width = kv_ref.shape[2]
    head_count = width // HD
    pages = kv_ref.shape[1]
    scale = 1.0 / math.sqrt(HD)
    q = q_ref[:, :, 0:width].astype(jnp.float32).reshape(n_src * rows, width)
    group = q_ref[:, :, width : width + 1].astype(jnp.float32).reshape(n_src * rows, 1)
    lane = lax.broadcasted_iota(jnp.int32, q.shape, 1)
    out_ref[...] = jnp.zeros(out_ref.shape, jnp.float32)
    for h in range(head_count):
        inside = (lane >= h * HD) & (lane < (h + 1) * HD)
        q_head = jnp.where(inside, q, 0.0).astype(jnp.bfloat16)
        scores = []
        masks = []
        top = jnp.full((n_src * rows, 1), NEG_FLOOR, jnp.float32)
        for k in range(pages):
            score = jnp.dot(q_head, kv_ref[0, k], preferred_element_type=jnp.float32) * scale
            mask = group == pg_ref[0:1, k : k + 1]
            top = jnp.maximum(top, jnp.max(jnp.where(mask, score, NEG_FLOOR), axis=1, keepdims=True))
            scores.append(score)
            masks.append(mask)
        total = jnp.zeros((n_src * rows, 1), jnp.float32)
        mixed = jnp.zeros((n_src * rows, HD), jnp.float32)
        for k in range(pages):
            weight = jnp.exp(jnp.where(masks[k], scores[k] - top, NEG_FLOOR))
            total = total + jnp.sum(weight, axis=1, keepdims=True)
            mixed = mixed + lax.dot_general(
                weight.astype(jnp.bfloat16),
                kv_ref[1, k, h * HD : (h + 1) * HD, :],
                (((1,), (1,)), ((), ())),
                preferred_element_type=jnp.float32,
            )
        out_ref[:, h, :, 0:HD] = mixed.reshape(n_src, rows, HD)
        out_ref[:, h, :, HD : HD + 1] = top.reshape(n_src, rows, 1)
        out_ref[:, h, :, HD + 1 : HD + 2] = total.reshape(n_src, rows, 1)


def page_partials(payload, page_group, layer_prompt, lanes):
    n_src, rows, _ = payload.shape
    width = layer_prompt.shape[2]
    groups = jnp.zeros((8, lanes), jnp.float32).at[0, : page_group.shape[0]].set(page_group.astype(jnp.float32))
    return pl.pallas_call(
        page_kernel,
        out_shape=jax.ShapeDtypeStruct((n_src, width // HD, rows, lanes), jnp.float32),
        in_specs=[pl.BlockSpec(memory_space=pltpu.VMEM)] * 3,
        out_specs=pl.BlockSpec(memory_space=pltpu.VMEM),
    )(payload, groups, layer_prompt)


def attend_project(payload, query, key_new, val_new, layer_suffix, layer_prompt, valid, page_group, n_req, w_layer):
    row_count = query.shape[0]
    head_count = query.shape[1] // HD
    scale = 1.0 / math.sqrt(HD)
    page_len = layer_suffix.shape[3]
    lanes = 128
    query_heads = query.reshape(row_count, head_count, HD)
    key_heads = key_new.reshape(row_count, head_count, HD)
    val_heads = val_new.reshape(row_count, head_count, HD)

    packed = page_partials(payload, page_group, layer_prompt, lanes)
    packed, query_heads = lax.optimization_barrier((packed, query_heads))
    back = send_home(packed, n_req)
    here = local_part(query_heads, key_new, val_new, layer_suffix, valid, lanes)
    return merge_project(back, here, w_layer)


def attend_gathered(query, key_new, val_new, layer_suffix, gathered_prompt, valid, group_id, prompt_owner, w_layer):
    row_count = query.shape[0]
    head_count = query.shape[1] // HD
    scale = 1.0 / math.sqrt(HD)
    page_len = layer_suffix.shape[3]
    lanes = 128
    query_heads = query.reshape(row_count, head_count, HD)
    here = local_part(query_heads, key_new, val_new, layer_suffix, valid, lanes)
    q_masked, inside = masked_queries(query, head_count)
    p_scores = (
        jnp.einsum("hif,kft->hikt", q_masked, gathered_prompt[0], preferred_element_type=jnp.float32)
        * scale
    )
    match = (group_id[:, None] == (prompt_owner // PPAGES)[None, :])[None, :, :, None]
    p_top, p_total, p_wide = softmax_part(
        p_scores,
        match,
        lambda w: jnp.einsum("hikt,kft->hif", w, gathered_prompt[1], preferred_element_type=jnp.float32),
        (2, 3),
    )
    p_mixed = own_head_features(p_wide, inside)
    back = pack_part(p_mixed, p_top, p_total, lanes)[None]
    return merge_project(back, here, w_layer)


def payload_of(query, group_id):
    return jnp.concatenate([query, group_id.astype(jnp.bfloat16)[:, None]], axis=1)


def make_local(n_req, n_head):
    def local(
        tokens,
        w_qkv,
        w_out,
        w_up,
        w_down,
        gain_attn,
        gain_mlp,
        suffix_cache,
        prompt_cache,
        suffix_table,
        prompt_owner,
        suffix_len,
        group_id,
    ):
        row_count = tokens.shape[0]
        layer_count = w_qkv.shape[0]
        width_here = w_qkv.shape[2]
        model_width = w_qkv.shape[3]
        page_len = suffix_cache.shape[4]
        pool = suffix_cache.shape[2]
        own_pages = suffix_table.shape[1] // row_count
        prompt_here = prompt_cache.shape[2]

        table = suffix_table[0].reshape(row_count, own_pages)
        rows = jnp.arange(page_len, dtype=jnp.int32)
        page_ids = jnp.arange(pool, dtype=jnp.int32)
        valid = jnp.zeros((row_count, pool, page_len), dtype=bool)
        for slot in range(own_pages):
            chosen = (table[:, slot][:, None] == page_ids[None, :])[:, :, None]
            filled = (slot * page_len + rows)[None, None, :] < suffix_len[:, None, None]
            valid = valid | (chosen & filled)

        here = lax.axis_index("req")
        page_group = lax.dynamic_slice(prompt_owner, (here * prompt_here,), (prompt_here,)) // PPAGES

        last_prompt = lax.all_gather(prompt_cache[layer_count - 1], "req", axis=1, tiled=True)
        whole = tokens.astype(jnp.float32)
        normed = root_norm(whole, gain_attn[0]).astype(jnp.bfloat16)
        residual = whole
        new_keys = []
        new_vals = []
        for layer in range(layer_count):
            projected = jnp.einsum(
                "rd,kd->rk",
                normed,
                w_qkv[layer].reshape(3 * width_here, model_width),
                preferred_element_type=jnp.float32,
            )
            projected = projected.reshape(row_count, 3, width_here).astype(jnp.bfloat16)
            query = projected[:, 0]
            key_new = projected[:, 1]
            val_new = projected[:, 2]
            new_keys.append(key_new)
            new_vals.append(val_new)
            if layer == layer_count - 1 and layer > 0:
                partial_value = attend_gathered(
                    query, key_new, val_new, suffix_cache[layer], last_prompt, valid,
                    group_id, prompt_owner, w_out[layer],
                )
            elif layer == 0:
                gathered = spread(payload_of(query, group_id), n_req)
            else:
                gathered = spread(payload_of(query, group_id), n_req)
            if layer < layer_count - 1 or layer == 0:
              partial_value = attend_project(
                gathered,
                query,
                key_new,
                val_new,
                suffix_cache[layer],
                prompt_cache[layer],
                valid,
                page_group,
                n_req,
                w_out[layer],
            )
            residual = residual + head_sum(partial_value, n_head)
            normed = root_norm(residual, gain_mlp[layer]).astype(jnp.bfloat16)
            hidden_units = jax.nn.silu(
                jnp.einsum("rd,fd->rf", normed, w_up[layer], preferred_element_type=jnp.float32)
            ).astype(jnp.bfloat16)
            partial_value = jnp.dot(hidden_units, w_down[layer], preferred_element_type=jnp.float32)
            residual = residual + head_sum(partial_value, n_head)
            if layer + 1 < layer_count:
                normed = root_norm(residual, gain_attn[layer + 1]).astype(jnp.bfloat16)
        hidden = residual.astype(jnp.bfloat16)
        new_cache = jnp.stack([jnp.stack(new_keys), jnp.stack(new_vals)], axis=1)
        return (hidden, new_cache)

    return local


def solution(mesh):
    placed = (
        P("req", None),
        P(None, None, "head", None),
        P(None, "head", None),
        P(None, "head", None),
        P(None, "head", None),
        P(),
        P(),
        P(None, None, "req", "head", None),
        P(None, None, "req", "head", None),
        P("req", None),
        P(),
        P("req"),
        P("req"),
    )
    return jax.shard_map(
        make_local(mesh.shape["req"], mesh.shape["head"]),
        mesh=mesh,
        in_specs=placed,
        out_specs=(P("req", None), P(None, None, "req", "head")),
        check_vma=False,
    )
```

```python
import math

import jax
import jax.numpy as jnp
from jax import lax
from jax.experimental import pallas as pl
from jax.experimental.pallas import tpu as pltpu
from jax.sharding import PartitionSpec as P

HD = 80
PPAGES = 4


NEG_FLOOR = -1e30


def root_norm(values, gains):
    factor = lax.rsqrt(jnp.mean(values * values, axis=-1, keepdims=True) + 1e-06)
    return values * factor * gains


def head_sum(value, count):
    chips = count // 2
    value = value + lax.ppermute(value, "head", [(i, i ^ 1) for i in range(count)])

    def from_chip(shift):
        pairs = [(i, ((i // 2 + shift) % chips) * 2 + i % 2) for i in range(count)]
        return lax.ppermute(value, "head", pairs)

    later = from_chip(1)
    opposite = from_chip(2)
    earlier = from_chip(chips - 1)
    return (value + opposite) + (later + earlier)


def spread(value, count):
    copies = jnp.broadcast_to(value[None], (count,) + value.shape)
    return lax.all_to_all(copies, "req", 0, 0, tiled=True)


def send_home(parts, count):
    return lax.all_to_all(parts, "req", 0, 0, tiled=True)


def softmax_part(scores, mask, values_fn, axes):
    top = jnp.max(jnp.where(mask, scores, NEG_FLOOR), axis=axes)
    expand = top.reshape(top.shape + (1,) * len(axes))
    weights = jnp.exp(jnp.where(mask, scores - expand, NEG_FLOOR))
    total = jnp.sum(weights, axis=axes)
    mixed = values_fn(weights.astype(jnp.bfloat16))
    return top, total, mixed


def pack_part(mixed, top, total, lanes):
    pad = jnp.zeros(mixed.shape[:-1] + (lanes - HD - 2,), jnp.float32)
    return jnp.concatenate([mixed, top[..., None], total[..., None], pad], axis=-1)


def merge_kernel(back_ref, here_ref, w_ref, out_ref):
    head_count = here_ref.shape[0]
    acc = jnp.zeros(out_ref.shape, jnp.float32)
    for h in range(head_count):
        back = back_ref[:, h]
        here = here_ref[h]
        b_top = back[:, :, HD : HD + 1]
        h_top = here[:, HD : HD + 1]
        top = jnp.maximum(jnp.max(b_top, axis=0), h_top)
        b_factor = jnp.exp(b_top - top[None])
        h_factor = jnp.exp(h_top - top)
        total = jnp.sum(back[:, :, HD + 1 : HD + 2] * b_factor, axis=0) + here[:, HD + 1 : HD + 2] * h_factor
        mixed = jnp.sum(back[:, :, :HD] * b_factor, axis=0) + here[:, :HD] * h_factor
        attended = (mixed / total).astype(jnp.bfloat16)
        acc = acc + jnp.dot(attended, w_ref[h * HD : (h + 1) * HD, :], preferred_element_type=jnp.float32)
    out_ref[...] = acc


def merge_project(back, here, w_layer):
    n_src, head_count, rows, lanes = back.shape
    width = w_layer.shape[1]
    return pl.pallas_call(
        merge_kernel,
        out_shape=jax.ShapeDtypeStruct((rows, width), jnp.float32),
        in_specs=[
            pl.BlockSpec(memory_space=pltpu.VMEM),
            pl.BlockSpec(memory_space=pltpu.VMEM),
            pl.BlockSpec(memory_space=pltpu.VMEM),
        ],
        out_specs=pl.BlockSpec(memory_space=pltpu.VMEM),
    )(back, here, w_layer)


def local_part(query_heads, key_new, val_new, layer_suffix, valid, lanes):
    row_count, head_count, _ = query_heads.shape
    scale = 1.0 / math.sqrt(HD)
    page_len = layer_suffix.shape[3]
    key_heads = key_new.reshape(row_count, head_count, HD)
    val_heads = val_new.reshape(row_count, head_count, HD)
    pool = layer_suffix.shape[1]
    s_keys = layer_suffix[0].reshape(pool, head_count, HD, page_len)
    s_vals = layer_suffix[1].reshape(pool, head_count, HD, page_len)
    s_scores = (
        jnp.einsum("ihd,phdt->ihpt", query_heads, s_keys, preferred_element_type=jnp.float32)
        * scale
    )
    s_top, s_total, s_mixed = softmax_part(
        s_scores,
        valid[:, None],
        lambda w: jnp.einsum("ihpt,phdt->ihd", w, s_vals, preferred_element_type=jnp.float32),
        (2, 3),
    )
    own = (
        jnp.einsum("rhd,rhd->rh", query_heads, key_heads, preferred_element_type=jnp.float32)
        * scale
    )
    l_top = jnp.maximum(s_top, own)
    s_factor = jnp.exp(s_top - l_top)
    own_weight = jnp.exp(own - l_top)
    l_total = s_total * s_factor + own_weight
    l_mixed = (
        s_mixed * s_factor[..., None]
        + own_weight.astype(jnp.bfloat16).astype(jnp.float32)[..., None]
        * val_heads.astype(jnp.float32)
    )
    return pack_part(l_mixed, l_top, l_total, lanes).transpose(1, 0, 2)


def page_kernel(q_ref, pg_ref, kv_ref, out_ref):
    n_src, rows, cols = q_ref.shape
    width = kv_ref.shape[2]
    head_count = width // HD
    pages = kv_ref.shape[1]
    scale = 1.0 / math.sqrt(HD)
    q = q_ref[:, :, 0:width].astype(jnp.float32).reshape(n_src * rows, width)
    group = q_ref[:, :, width : width + 1].astype(jnp.float32).reshape(n_src * rows, 1)
    lane = lax.broadcasted_iota(jnp.int32, q.shape, 1)
    for h in range(head_count):
        inside = (lane >= h * HD) & (lane < (h + 1) * HD)
        q_head = jnp.where(inside, q, 0.0).astype(jnp.bfloat16)
        scores = []
        masks = []
        top = jnp.full((n_src * rows, 1), NEG_FLOOR, jnp.float32)
        for k in range(pages):
            score = jnp.dot(q_head, kv_ref[0, k], preferred_element_type=jnp.float32) * scale
            mask = group == pg_ref[0:1, k : k + 1]
            top = jnp.maximum(top, jnp.max(jnp.where(mask, score, NEG_FLOOR), axis=1, keepdims=True))
            scores.append(score)
            masks.append(mask)
        total = jnp.zeros((n_src * rows, 1), jnp.float32)
        mixed = jnp.zeros((n_src * rows, HD), jnp.float32)
        for k in range(pages):
            weight = jnp.exp(jnp.where(masks[k], scores[k] - top, NEG_FLOOR))
            total = total + jnp.sum(weight, axis=1, keepdims=True)
            mixed = mixed + lax.dot_general(
                weight.astype(jnp.bfloat16),
                kv_ref[1, k, h * HD : (h + 1) * HD, :],
                (((1,), (1,)), ((), ())),
                preferred_element_type=jnp.float32,
            )
        out_ref[:, h, :, 0:HD] = mixed.reshape(n_src, rows, HD)
        out_ref[:, h, :, HD : HD + 1] = top.reshape(n_src, rows, 1)
        out_ref[:, h, :, HD + 1 : HD + 2] = total.reshape(n_src, rows, 1)


def page_partials(payload, page_group, layer_prompt, lanes):
    n_src, rows, _ = payload.shape
    width = layer_prompt.shape[2]
    groups = jnp.zeros((8, lanes), jnp.float32).at[0, : page_group.shape[0]].set(page_group.astype(jnp.float32))
    return pl.pallas_call(
        page_kernel,
        out_shape=jax.ShapeDtypeStruct((n_src, width // HD, rows, lanes), jnp.float32),
        in_specs=[pl.BlockSpec(memory_space=pltpu.VMEM)] * 3,
        out_specs=pl.BlockSpec(memory_space=pltpu.VMEM),
    )(payload, groups, layer_prompt)


def attend_project(payload, query, key_new, val_new, layer_suffix, layer_prompt, valid, page_group, n_req, w_layer):
    row_count = query.shape[0]
    head_count = query.shape[1] // HD
    scale = 1.0 / math.sqrt(HD)
    page_len = layer_suffix.shape[3]
    lanes = 128
    query_heads = query.reshape(row_count, head_count, HD)
    key_heads = key_new.reshape(row_count, head_count, HD)
    val_heads = val_new.reshape(row_count, head_count, HD)

    here = local_part(query_heads, key_new, val_new, layer_suffix, valid, lanes)

    packed = page_partials(payload, page_group, layer_prompt, lanes)
    back = send_home(packed, n_req)
    return merge_project(back, here, w_layer)


def attend_gathered(query, key_new, val_new, layer_suffix, gathered_prompt, valid, group_id, prompt_owner, w_layer):
    row_count = query.shape[0]
    head_count = query.shape[1] // HD
    scale = 1.0 / math.sqrt(HD)
    page_len = layer_suffix.shape[3]
    lanes = 128
    query_heads = query.reshape(row_count, head_count, HD)
    here = local_part(query_heads, key_new, val_new, layer_suffix, valid, lanes)
    width = query.shape[1]
    lane_head = jnp.arange(width, dtype=jnp.int32) // HD
    heads = jnp.arange(head_count, dtype=jnp.int32)
    inside = lane_head[None, :] == heads[:, None]
    q_masked = jnp.where(inside[:, None, :], query[None], jnp.zeros((), query.dtype))
    p_scores = (
        jnp.einsum("hif,kft->hikt", q_masked, gathered_prompt[0], preferred_element_type=jnp.float32)
        * scale
    )
    match = (group_id[:, None] == (prompt_owner // PPAGES)[None, :])[None, :, :, None]
    p_top, p_total, p_wide = softmax_part(
        p_scores,
        match,
        lambda w: jnp.einsum("hikt,kft->hif", w, gathered_prompt[1], preferred_element_type=jnp.float32),
        (2, 3),
    )
    p_mixed = jnp.sum(jnp.where(inside[:, None, :], p_wide, 0.0).reshape(head_count, row_count, head_count, HD), axis=2)
    back = pack_part(p_mixed, p_top, p_total, lanes)[None]
    return merge_project(back, here, w_layer)


def payload_of(query, group_id):
    return jnp.concatenate([query, group_id.astype(jnp.bfloat16)[:, None]], axis=1)


def make_local(n_req, n_head):
    def local(
        tokens,
        w_qkv,
        w_out,
        w_up,
        w_down,
        gain_attn,
        gain_mlp,
        suffix_cache,
        prompt_cache,
        suffix_table,
        prompt_owner,
        suffix_len,
        group_id,
    ):
        row_count = tokens.shape[0]
        layer_count = w_qkv.shape[0]
        width_here = w_qkv.shape[2]
        model_width = w_qkv.shape[3]
        page_len = suffix_cache.shape[4]
        pool = suffix_cache.shape[2]
        own_pages = suffix_table.shape[1] // row_count
        prompt_here = prompt_cache.shape[2]

        table = suffix_table[0].reshape(row_count, own_pages)
        rows = jnp.arange(page_len, dtype=jnp.int32)
        page_ids = jnp.arange(pool, dtype=jnp.int32)
        valid = jnp.zeros((row_count, pool, page_len), dtype=bool)
        for slot in range(own_pages):
            chosen = (table[:, slot][:, None] == page_ids[None, :])[:, :, None]
            filled = (slot * page_len + rows)[None, None, :] < suffix_len[:, None, None]
            valid = valid | (chosen & filled)

        here = lax.axis_index("req")
        page_group = lax.dynamic_slice(prompt_owner, (here * prompt_here,), (prompt_here,)) // PPAGES

        last_prompt = lax.all_gather(prompt_cache[layer_count - 1], "req", axis=1, tiled=True)
        whole = tokens.astype(jnp.float32)
        normed = root_norm(whole, gain_attn[0]).astype(jnp.bfloat16)
        residual = whole
        new_keys = []
        new_vals = []
        for layer in range(layer_count):
            projected = jnp.einsum(
                "rd,kd->rk",
                normed,
                w_qkv[layer].reshape(3 * width_here, model_width),
                preferred_element_type=jnp.float32,
            )
            projected = projected.reshape(row_count, 3, width_here).astype(jnp.bfloat16)
            query = projected[:, 0]
            key_new = projected[:, 1]
            val_new = projected[:, 2]
            new_keys.append(key_new)
            new_vals.append(val_new)
            if layer == layer_count - 1 and layer > 0:
                partial_value = attend_gathered(
                    query, key_new, val_new, suffix_cache[layer], last_prompt, valid,
                    group_id, prompt_owner, w_out[layer],
                )
            elif layer == 0:
                gathered = spread(payload_of(query, group_id), n_req)
            else:
                gathered = spread(payload_of(query, group_id), n_req)
            if layer < layer_count - 1 or layer == 0:
              partial_value = attend_project(
                gathered,
                query,
                key_new,
                val_new,
                suffix_cache[layer],
                prompt_cache[layer],
                valid,
                page_group,
                n_req,
                w_out[layer],
            )
            residual = residual + head_sum(partial_value, n_head)
            normed = root_norm(residual, gain_mlp[layer]).astype(jnp.bfloat16)
            hidden_units = jax.nn.silu(
                jnp.einsum("rd,fd->rf", normed, w_up[layer], preferred_element_type=jnp.float32)
            ).astype(jnp.bfloat16)
            partial_value = jnp.dot(hidden_units, w_down[layer], preferred_element_type=jnp.float32)
            residual = residual + head_sum(partial_value, n_head)
            if layer + 1 < layer_count:
                normed = root_norm(residual, gain_attn[layer + 1]).astype(jnp.bfloat16)
        hidden = residual.astype(jnp.bfloat16)
        new_cache = jnp.stack([jnp.stack(new_keys), jnp.stack(new_vals)], axis=1)
        return (hidden, new_cache)

    return local


def solution(mesh):
    placed = (
        P("req", None),
        P(None, None, "head", None),
        P(None, "head", None),
        P(None, "head", None),
        P(None, "head", None),
        P(),
        P(),
        P(None, None, "req", "head", None),
        P(None, None, "req", "head", None),
        P("req", None),
        P(),
        P("req"),
        P("req"),
    )
    return jax.shard_map(
        make_local(mesh.shape["req"], mesh.shape["head"]),
        mesh=mesh,
        in_specs=placed,
        out_specs=(P("req", None), P(None, None, "req", "head")),
        check_vma=False,
    )
```
